256 devices in a mesh: blk: 32 (over x_lo, z, core), tp: 8 (over y, x_hi).
Axes of the slice: x: 4 (x_hi: 2, x_lo: 2; x = x_hi * 2 + x_lo), y: 4, z: 8, core: 2. Of those that a mesh axis runs over, the one named last changes fastest.
Arguments:
- hidden_in: bfloat16 [12288, 4096], P('blk'), may hold values from -6 to 6
- w_query: bfloat16 [4096, 4096], P('blk', 'tp'), may hold values from -0.09375 to 0.09375
- w_key: bfloat16 [4096, 1024], P('blk', 'tp'), may hold values from -0.09375 to 0.09375
- w_value: bfloat16 [4096, 1024], P('blk', 'tp'), may hold values from -0.09375 to 0.09375
- starts: int32 [32], P('blk'), may hold values from 0 to 1152, as said below
- key_cache: bfloat16 [32, 1152, 1024], P('blk', None, 'tp'), may hold values from -400 to 400
- value_cache: bfloat16 [32, 1152, 1024], P('blk', None, 'tp'), may hold values from -6 to 6
- grad_out: bfloat16 [12288, 4096], P('blk', 'tp'), may hold values from -6 to 6
Outputs:
- attended: bfloat16 [12288, 4096], P('blk', 'tp')
- grad_in: bfloat16 [12288, 4096], P('blk', 'tp')
- grad_wq: float32 [4096, 4096], P('blk', 'tp')
- grad_wk: float32 [4096, 1024], P('blk', 'tp')
- grad_wv: float32 [4096, 1024], P('blk', 'tp')
The draws below stay inside these ranges and needn't reach their ends.
Inputs may be any that keep to these rules, and one draw needn't show every extreme that they name: `starts`: every entry is a multiple of 384; both 0 and 1152 occur.
All inputs are finite; a program needn't handle non-finite values.
Results may differ from the reference program's by a relative error of at most 0.025.
The reference program's roundings to bfloat16 on the way count: a program that leaves them out, or rounds other values in their place, can miss the bound.
Values may be sent and summed in bfloat16 or wider, within the bound.
No kernel may reach another device: no remote copies, remote signals or barrier semaphores. Data moves between devices by JAX's collectives and lax.ppermute only.
A program may use at most 128 MiB of HBM per device.

```python
import jax
import jax.numpy as jnp
from jax import lax

D = 4096
H = 32
KV = 8
HD = 128
TOK_DEV = 384
CACHE_BLOCKS = 3
CACHE = 1152
TOKENS = 12288
N_BLK = 32


def draw_starts(key, part):
    order = jax.random.permutation(key, N_BLK)
    return (order % (CACHE_BLOCKS + 1) * TOK_DEV).astype(jnp.int32)


def draw_key_cache(key, part):
    base = jnp.clip(jax.random.normal(key, (N_BLK, CACHE, KV * HD), jnp.float32), -4.0, 4.0)
    return base.astype(jnp.bfloat16)


def with_spikes(result, key, source, target, shards_of, factor):
    owner, partner = [(jnp.arange(result.shape[dim]) // (result.shape[dim] // shards_of)).reshape([-1 if axis == dim else 1 for axis in range(result.ndim)]) for dim in (source, target)]
    chosen = jax.random.permutation(key, shards_of)[partner]
    strong = (owner == chosen) | (owner == (partner + shards_of // 2) % shards_of)
    return jnp.where(strong, factor * result, result)


def block_scale(own_key, extent, cuts, least, high):
    loudness, own = 1.0, jax.random.fold_in(own_key, 6)
    for position, blocks in cuts:
        steps = jnp.exp(jax.random.uniform(jax.random.fold_in(own, position), (blocks,), jnp.float32, least / len(cuts), high / len(cuts)))
        loudness = loudness * jnp.repeat(steps, extent[position] // blocks).reshape([-1 if axis == position else 1 for axis in range(len(extent))])
    return loudness


def centred(rng, extent, deviation, limit, split=(), held_as=jnp.bfloat16):
    gain = block_scale(rng, extent, split, -0.22, 0.18) if split else 1.0
    result = jax.random.normal(rng, extent, jnp.float32) * deviation * gain
    return jnp.minimum(jnp.maximum(result, -limit), limit).astype(held_as)


def gaussian_with(own_key, shape, deviation, reach, cuts, heavy, kind=jnp.bfloat16):
    entries = deviation * jax.random.normal(own_key, shape, jnp.float32)
    if cuts:
        entries = entries * block_scale(own_key, shape, cuts, -0.22, 0.18)
    return jnp.clip(with_spikes(entries, jax.random.fold_in(own_key, 3), *heavy), -reach, reach).astype(kind)


def setup_inputs(seed: int = 0) -> dict:
    key_of = jax.random.split(jax.random.key(seed), 9)
    hidden_in = gaussian_with(key_of[0], (TOKENS, D), 1.0, 6.0, ((0, 32),), (0, 1, 32, 2.75))
    w_query = centred(key_of[1], (D, H * HD), D ** -0.5, 0.09375, ((0, 32), (1, 8)))
    w_key = centred(key_of[2], (D, KV * HD), D ** -0.5, 0.09375, ((0, 32), (1, 8)))
    w_value = centred(key_of[3], (D, KV * HD), D ** -0.5, 0.09375, ((0, 32), (1, 8)))
    starts = draw_starts(jax.random.fold_in(key_of[8], 71), 0)
    key_cache = draw_key_cache(jax.random.fold_in(key_of[8], 71), 0)
    value_cache = centred(key_of[6], (N_BLK, CACHE, KV * HD), 1.0, 6.0, ((0, 32), (2, 8)))
    grad_out = centred(key_of[7], (TOKENS, H * HD), 1.0, 6.0, ((0, 32), (1, 8)))
    return {"hidden_in": hidden_in, "w_query": w_query, "w_key": w_key, "w_value": w_value, "starts": starts, "key_cache": key_cache, "value_cache": value_cache, "grad_out": grad_out}


def contract_last(left, right):
    return lax.dot_general(left, right, (((1,), (1,)), ((), ())), preferred_element_type=jnp.float32)


def contract_first(left, right):
    return lax.dot_general(left, right, (((0,), (0,)), ((), ())), preferred_element_type=jnp.float32)


def head_pass(queries, cache_keys, cache_values, fresh_keys, fresh_values, grad_heads, offset):
    groups, row_count, head_width = queries.shape
    cached = cache_keys.shape[0]
    factor = head_width ** -0.5
    key_list = jnp.concatenate([cache_keys, fresh_keys], 0)
    value_list = jnp.concatenate([cache_values, fresh_values], 0)
    flat_query = queries.reshape(groups * row_count, head_width)
    flat_grad = grad_heads.reshape(groups * row_count, head_width)
    scores = contract_last(flat_query, key_list) * factor
    scores = scores.reshape(groups, row_count, cached + row_count)
    row_pos = lax.iota(jnp.int32, row_count)
    cache_ok = jnp.broadcast_to(lax.iota(jnp.int32, cached)[None, :] < offset, (row_count, cached))
    own_ok = row_pos[None, :] <= row_pos[:, None]
    allowed = jnp.concatenate([cache_ok, own_ok], 1)
    scores = jnp.where(allowed[None], scores, -jnp.inf)
    row_max = jnp.max(scores, axis=-1, keepdims=True)
    expo = jnp.exp(scores - row_max)
    probs = (expo / jnp.sum(expo, axis=-1, keepdims=True)).astype(jnp.bfloat16)
    probs = probs.reshape(groups * row_count, cached + row_count)
    attended = jnp.dot(probs, value_list, preferred_element_type=jnp.float32).astype(jnp.bfloat16)
    grad_probs = contract_last(flat_grad, value_list)
    probs_wide = probs.astype(jnp.float32)
    row_dot = jnp.sum(probs_wide * grad_probs, axis=-1, keepdims=True)
    grad_scores = (probs_wide * (grad_probs - row_dot) * factor).astype(jnp.bfloat16)
    grad_query = jnp.dot(grad_scores, key_list, preferred_element_type=jnp.float32).astype(jnp.bfloat16)
    grad_keys = contract_first(grad_scores[:, cached:], flat_query).astype(jnp.bfloat16)
    grad_values = contract_first(probs[:, cached:], flat_grad).astype(jnp.bfloat16)
    return (attended.reshape(groups, row_count, head_width), grad_query.reshape(groups, row_count, head_width), grad_keys, grad_values)


def reference(hidden_in, w_query, w_key, w_value, starts, key_cache, value_cache, grad_out):
    group = H // KV
    queries = jnp.dot(hidden_in, w_query, preferred_element_type=jnp.float32).astype(jnp.bfloat16)
    new_keys = jnp.dot(hidden_in, w_key, preferred_element_type=jnp.float32).astype(jnp.bfloat16)
    new_values = jnp.dot(hidden_in, w_value, preferred_element_type=jnp.float32).astype(jnp.bfloat16)
    per_query = queries.reshape(N_BLK, TOK_DEV, KV, group, HD).transpose(0, 2, 3, 1, 4)
    per_grad = grad_out.reshape(N_BLK, TOK_DEV, KV, group, HD).transpose(0, 2, 3, 1, 4)
    cache_k = key_cache.reshape(N_BLK, CACHE, KV, HD).transpose(0, 2, 1, 3)
    cache_v = value_cache.reshape(N_BLK, CACHE, KV, HD).transpose(0, 2, 1, 3)
    fresh_k = new_keys.reshape(N_BLK, TOK_DEV, KV, HD).transpose(0, 2, 1, 3)
    fresh_v = new_values.reshape(N_BLK, TOK_DEV, KV, HD).transpose(0, 2, 1, 3)

    def per_block(packed):
        offset = packed[6]
        return lax.map(lambda inner: head_pass(*inner, offset), packed[:6])

    results = lax.map(per_block, (per_query, cache_k, cache_v, fresh_k, fresh_v, per_grad, starts))
    attended = results[0].transpose(0, 3, 1, 2, 4).reshape(TOKENS, H * HD)
    grad_query = results[1].transpose(0, 3, 1, 2, 4).reshape(TOKENS, H * HD)
    grad_keys = results[2].transpose(0, 2, 1, 3).reshape(TOKENS, KV * HD)
    grad_values = results[3].transpose(0, 2, 1, 3).reshape(TOKENS, KV * HD)
    grad_in = (contract_last(grad_query, w_query) + contract_last(grad_keys, w_key) + contract_last(grad_values, w_value)).astype(jnp.bfloat16)
    factor = TOKENS ** -0.5
    grad_wq = contract_first(hidden_in, grad_query) * factor
    grad_wk = contract_first(hidden_in, grad_keys) * factor
    grad_wv = contract_first(hidden_in, grad_values) * factor
    return (attended, grad_in, grad_wq, grad_wk, grad_wv)
```

```python
import jax
import jax.numpy as jnp
from jax import lax
from jax.sharding import PartitionSpec as P

H = 32
KV = 8
HD = 128


def contract_last(left, right):
    return lax.dot_general(
        left, right, (((1,), (1,)), ((), ())), preferred_element_type=jnp.float32
    )


def contract_first(left, right):
    return lax.dot_general(
        left, right, (((0,), (0,)), ((), ())), preferred_element_type=jnp.float32
    )


def head_pass(queries, cache_keys, cache_values, fresh_keys, fresh_values, grad_heads, offset):
    groups, row_count, head_width = queries.shape
    cached = cache_keys.shape[0]
    factor = head_width ** (-0.5)
    key_list = jnp.concatenate([cache_keys, fresh_keys], 0)
    value_list = jnp.concatenate([cache_values, fresh_values], 0)
    flat_query = queries.reshape(groups * row_count, head_width)
    flat_grad = grad_heads.reshape(groups * row_count, head_width)
    scores = contract_last(flat_query, key_list) * factor
    scores = scores.reshape(groups, row_count, cached + row_count)
    row_pos = lax.iota(jnp.int32, row_count)
    cache_ok = jnp.broadcast_to(lax.iota(jnp.int32, cached)[None, :] < offset, (row_count, cached))
    own_ok = row_pos[None, :] <= row_pos[:, None]
    allowed = jnp.concatenate([cache_ok, own_ok], 1)
    scores = jnp.where(allowed[None], scores, -jnp.inf)
    row_max = jnp.max(scores, axis=-1, keepdims=True)
    expo = jnp.exp(scores - row_max)
    probs = (expo / jnp.sum(expo, axis=-1, keepdims=True)).astype(jnp.bfloat16)
    probs = probs.reshape(groups * row_count, cached + row_count)
    attended = jnp.dot(probs, value_list, preferred_element_type=jnp.float32).astype(jnp.bfloat16)
    grad_probs = contract_last(flat_grad, value_list)
    probs_wide = probs.astype(jnp.float32)
    row_dot = jnp.sum(probs_wide * grad_probs, axis=-1, keepdims=True)
    grad_scores = (probs_wide * (grad_probs - row_dot) * factor).astype(jnp.bfloat16)
    grad_query = jnp.dot(grad_scores, key_list, preferred_element_type=jnp.float32).astype(
        jnp.bfloat16
    )
    grad_keys = contract_first(grad_scores[:, cached:], flat_query).astype(jnp.bfloat16)
    grad_values = contract_first(probs[:, cached:], flat_grad).astype(jnp.bfloat16)
    return (
        attended.reshape(groups, row_count, head_width),
        grad_query.reshape(groups, row_count, head_width),
        grad_keys,
        grad_values,
    )


def local(hidden_in, w_query, w_key, w_value, starts, key_cache, value_cache, grad_out):
    tokens_dev = hidden_in.shape[0]
    kv_local = w_key.shape[1] // HD
    group = H // KV
    cached = key_cache.shape[1]
    query_cols = w_query.shape[1]
    kv_cols = w_key.shape[1]
    local_w = jnp.concatenate([w_query, w_key, w_value], 1)
    full_w = lax.all_gather(local_w, "blk", axis=0, tiled=True)
    proj = jnp.dot(hidden_in, full_w, preferred_element_type=jnp.float32)
    queries = proj[:, :query_cols].astype(jnp.bfloat16)
    new_keys = proj[:, query_cols : query_cols + kv_cols].astype(jnp.bfloat16)
    new_values = proj[:, query_cols + kv_cols :].astype(jnp.bfloat16)
    per_query = queries.reshape(tokens_dev, kv_local, group, HD).transpose(1, 2, 0, 3)
    per_grad = grad_out.reshape(tokens_dev, kv_local, group, HD).transpose(1, 2, 0, 3)
    cache_k = key_cache[0].reshape(cached, kv_local, HD).transpose(1, 0, 2)
    cache_v = value_cache[0].reshape(cached, kv_local, HD).transpose(1, 0, 2)
    fresh_k = new_keys.reshape(tokens_dev, kv_local, HD).transpose(1, 0, 2)
    fresh_v = new_values.reshape(tokens_dev, kv_local, HD).transpose(1, 0, 2)
    offset = starts[0]
    results = lax.map(
        lambda packed: head_pass(*packed, offset),
        (per_query, cache_k, cache_v, fresh_k, fresh_v, per_grad),
    )
    attended = results[0].transpose(2, 0, 1, 3).reshape(tokens_dev, kv_local * group * HD)
    grad_query = results[1].transpose(2, 0, 1, 3).reshape(tokens_dev, kv_local * group * HD)
    grad_keys = results[2].transpose(1, 0, 2).reshape(tokens_dev, kv_local * HD)
    grad_values = results[3].transpose(1, 0, 2).reshape(tokens_dev, kv_local * HD)
    grads_cat = jnp.concatenate([grad_query, grad_keys, grad_values], 1)
    input_term = contract_last(grads_cat, full_w)
    grad_in = lax.psum_scatter(input_term, "tp", scatter_dimension=1, tiled=True).astype(
        jnp.bfloat16
    )
    blk_count = lax.axis_size("blk")
    summed = lax.psum_scatter(
        contract_first(hidden_in, grads_cat), "blk", scatter_dimension=0, tiled=True
    )
    summed = summed * (tokens_dev * blk_count) ** (-0.5)
    grad_wq = summed[:, :query_cols]
    grad_wk = summed[:, query_cols : query_cols + kv_cols]
    grad_wv = summed[:, query_cols + kv_cols :]
    return (attended, grad_in, grad_wq, grad_wk, grad_wv)


def solution(mesh):
    in_specs = (
        P("blk", None),
        P("blk", "tp"),
        P("blk", "tp"),
        P("blk", "tp"),
        P("blk"),
        P("blk", None, "tp"),
        P("blk", None, "tp"),
        P("blk", "tp"),
    )
    out_specs = (P("blk", "tp"), P("blk", "tp"), P("blk", "tp"), P("blk", "tp"), P("blk", "tp"))
    return jax.shard_map(local, mesh=mesh, in_specs=in_specs, out_specs=out_specs, check_vma=False)
```

```python
import jax
import jax.numpy as jnp
from jax import lax
from jax.sharding import PartitionSpec as P

H = 32
KV = 8
HD = 128


def contract_last(left, right):
    return lax.dot_general(
        left, right, (((1,), (1,)), ((), ())), preferred_element_type=jnp.float32
    )


def contract_first(left, right):
    return lax.dot_general(
        left, right, (((0,), (0,)), ((), ())), preferred_element_type=jnp.float32
    )


def head_pass(queries, cache_keys, cache_values, fresh_keys, fresh_values, grad_heads, offset):
    groups, row_count, head_width = queries.shape
    cached = cache_keys.shape[0]
    factor = head_width ** (-0.5)
    key_list = jnp.concatenate([cache_keys, fresh_keys], 0)
    value_list = jnp.concatenate([cache_values, fresh_values], 0)
    flat_query = queries.reshape(groups * row_count, head_width)
    flat_grad = grad_heads.reshape(groups * row_count, head_width)
    scores = contract_last(flat_query, key_list) * factor
    scores = scores.reshape(groups, row_count, cached + row_count)
    row_pos = lax.iota(jnp.int32, row_count)
    cache_ok = jnp.broadcast_to(lax.iota(jnp.int32, cached)[None, :] < offset, (row_count, cached))
    own_ok = row_pos[None, :] <= row_pos[:, None]
    allowed = jnp.concatenate([cache_ok, own_ok], 1)
    scores = jnp.where(allowed[None], scores, -jnp.inf)
    row_max = jnp.max(scores, axis=-1, keepdims=True)
    expo = jnp.exp(scores - row_max)
    probs = (expo / jnp.sum(expo, axis=-1, keepdims=True)).astype(jnp.bfloat16)
    probs = probs.reshape(groups * row_count, cached + row_count)
    attended = jnp.dot(probs, value_list, preferred_element_type=jnp.float32).astype(jnp.bfloat16)
    grad_probs = contract_last(flat_grad, value_list)
    probs_wide = probs.astype(jnp.float32)
    row_dot = jnp.sum(probs_wide * grad_probs, axis=-1, keepdims=True)
    grad_scores = (probs_wide * (grad_probs - row_dot) * factor).astype(jnp.bfloat16)
    grad_query = jnp.dot(grad_scores, key_list, preferred_element_type=jnp.float32).astype(
        jnp.bfloat16
    )
    grad_keys = contract_first(grad_scores[:, cached:], flat_query).astype(jnp.bfloat16)
    grad_values = contract_first(probs[:, cached:], flat_grad).astype(jnp.bfloat16)
    return (
        attended.reshape(groups, row_count, head_width),
        grad_query.reshape(groups, row_count, head_width),
        grad_keys,
        grad_values,
    )


def local(hidden_in, w_query, w_key, w_value, starts, key_cache, value_cache, grad_out):
    tokens_dev = hidden_in.shape[0]
    kv_local = w_key.shape[1] // HD
    group = H // KV
    cached = key_cache.shape[1]
    query_cols = w_query.shape[1]
    kv_cols = w_key.shape[1]
    local_w = jnp.concatenate([w_query, w_key, w_value], 1)
    full_w = lax.all_gather(local_w, "blk", axis=0, tiled=True)
    proj = jnp.dot(hidden_in, full_w, preferred_element_type=jnp.float32)
    queries = proj[:, :query_cols].astype(jnp.bfloat16)
    new_keys = proj[:, query_cols : query_cols + kv_cols].astype(jnp.bfloat16)
    new_values = proj[:, query_cols + kv_cols :].astype(jnp.bfloat16)
    per_query = queries.reshape(tokens_dev, kv_local, group, HD).transpose(1, 2, 0, 3)
    per_grad = grad_out.reshape(tokens_dev, kv_local, group, HD).transpose(1, 2, 0, 3)
    cache_k = key_cache[0].reshape(cached, kv_local, HD).transpose(1, 0, 2)
    cache_v = value_cache[0].reshape(cached, kv_local, HD).transpose(1, 0, 2)
    fresh_k = new_keys.reshape(tokens_dev, kv_local, HD).transpose(1, 0, 2)
    fresh_v = new_values.reshape(tokens_dev, kv_local, HD).transpose(1, 0, 2)
    offset = starts[0]
    results = lax.map(
        lambda packed: head_pass(*packed, offset),
        (per_query, cache_k, cache_v, fresh_k, fresh_v, per_grad),
    )
    attended = results[0].transpose(2, 0, 1, 3).reshape(tokens_dev, kv_local * group * HD)
    grad_query = results[1].transpose(2, 0, 1, 3).reshape(tokens_dev, kv_local * group * HD)
    grad_keys = results[2].transpose(1, 0, 2).reshape(tokens_dev, kv_local * HD)
    grad_values = results[3].transpose(1, 0, 2).reshape(tokens_dev, kv_local * HD)
    grads_cat = jnp.concatenate([grad_query, grad_keys, grad_values], 1)
    blk_count = lax.axis_size("blk")
    tp_count = lax.axis_size("tp")
    weight_term = contract_first(hidden_in, grads_cat).astype(jnp.bfloat16)
    summed = lax.psum_scatter(weight_term, "blk", scatter_dimension=0, tiled=True)
    summed = summed.astype(jnp.float32)
    input_term = contract_last(grads_cat, full_w).astype(jnp.bfloat16)
    input_term = input_term.reshape(tokens_dev, tp_count, -1).transpose(1, 0, 2)
    gathered = lax.all_to_all(input_term, "tp", 0, 0, tiled=True)
    grad_in = jnp.sum(gathered.astype(jnp.float32), axis=0).astype(jnp.bfloat16)
    summed = summed * (tokens_dev * blk_count) ** (-0.5)
    grad_wq = summed[:, :query_cols]
    grad_wk = summed[:, query_cols : query_cols + kv_cols]
    grad_wv = summed[:, query_cols + kv_cols :]
    return (attended, grad_in, grad_wq, grad_wk, grad_wv)


def solution(mesh):
    in_specs = (
        P("blk", None),
        P("blk", "tp"),
        P("blk", "tp"),
        P("blk", "tp"),
        P("blk"),
        P("blk", None, "tp"),
        P("blk", None, "tp"),
        P("blk", "tp"),
    )
    out_specs = (P("blk", "tp"), P("blk", "tp"), P("blk", "tp"), P("blk", "tp"), P("blk", "tp"))
    return jax.shard_map(local, mesh=mesh, in_specs=in_specs, out_specs=out_specs, check_vma=False)
```

```python
import jax
import jax.numpy as jnp
from jax import lax
from jax.sharding import Mesh, PartitionSpec as P

H = 32
KV = 8
HD = 128
SWAP = [(0, 1), (1, 0)]
BLK = ("xl", "z", "c")


def contract_last(left, right):
    return lax.dot_general(
        left, right, (((1,), (1,)), ((), ())), preferred_element_type=jnp.float32
    )


def contract_first(left, right):
    return lax.dot_general(
        left, right, (((0,), (0,)), ((), ())), preferred_element_type=jnp.float32
    )


def head_pass(queries, cache_keys, cache_values, fresh_keys, fresh_values, grad_heads, offset):
    groups, row_count, head_width = queries.shape
    cached = cache_keys.shape[0]
    factor = head_width ** (-0.5)
    key_list = jnp.concatenate([cache_keys, fresh_keys], 0)
    value_list = jnp.concatenate([cache_values, fresh_values], 0)
    flat_query = queries.reshape(groups * row_count, head_width)
    flat_grad = grad_heads.reshape(groups * row_count, head_width)
    scores = contract_last(flat_query, key_list) * factor
    scores = scores.reshape(groups, row_count, cached + row_count)
    row_pos = lax.iota(jnp.int32, row_count)
    cache_ok = jnp.broadcast_to(lax.iota(jnp.int32, cached)[None, :] < offset, (row_count, cached))
    own_ok = row_pos[None, :] <= row_pos[:, None]
    allowed = jnp.concatenate([cache_ok, own_ok], 1)
    scores = jnp.where(allowed[None], scores, -jnp.inf)
    row_max = jnp.max(scores, axis=-1, keepdims=True)
    expo = jnp.exp(scores - row_max)
    probs = (expo / jnp.sum(expo, axis=-1, keepdims=True)).astype(jnp.bfloat16)
    probs = probs.reshape(groups * row_count, cached + row_count)
    attended = jnp.dot(probs, value_list, preferred_element_type=jnp.float32).astype(jnp.bfloat16)
    grad_probs = contract_last(flat_grad, value_list)
    probs_wide = probs.astype(jnp.float32)
    row_dot = jnp.sum(probs_wide * grad_probs, axis=-1, keepdims=True)
    grad_scores = (probs_wide * (grad_probs - row_dot) * factor).astype(jnp.bfloat16)
    grad_query = jnp.dot(grad_scores, key_list, preferred_element_type=jnp.float32).astype(
        jnp.bfloat16
    )
    grad_keys = contract_first(grad_scores[:, cached:], flat_query).astype(jnp.bfloat16)
    grad_values = contract_first(probs[:, cached:], flat_grad).astype(jnp.bfloat16)
    return (
        attended.reshape(groups, row_count, head_width),
        grad_query.reshape(groups, row_count, head_width),
        grad_keys,
        grad_values,
    )


def local(hidden_in, w_query, w_key, w_value, starts, key_cache, value_cache, grad_out):
    tokens_dev = hidden_in.shape[0]
    kv_local = w_key.shape[1] // HD
    group = H // KV
    cached = key_cache.shape[1]
    query_cols = w_query.shape[1]
    kv_cols = w_key.shape[1]
    local_w = jnp.concatenate([w_query, w_key, w_value], 1)
    full_w = lax.all_gather(local_w, BLK, axis=0, tiled=True)
    proj = jnp.dot(hidden_in, full_w, preferred_element_type=jnp.float32)
    queries = proj[:, :query_cols].astype(jnp.bfloat16)
    new_keys = proj[:, query_cols : query_cols + kv_cols].astype(jnp.bfloat16)
    new_values = proj[:, query_cols + kv_cols :].astype(jnp.bfloat16)
    per_query = queries.reshape(tokens_dev, kv_local, group, HD).transpose(1, 2, 0, 3)
    per_grad = grad_out.reshape(tokens_dev, kv_local, group, HD).transpose(1, 2, 0, 3)
    cache_k = key_cache[0].reshape(cached, kv_local, HD).transpose(1, 0, 2)
    cache_v = value_cache[0].reshape(cached, kv_local, HD).transpose(1, 0, 2)
    fresh_k = new_keys.reshape(tokens_dev, kv_local, HD).transpose(1, 0, 2)
    fresh_v = new_values.reshape(tokens_dev, kv_local, HD).transpose(1, 0, 2)
    offset = starts[0]
    results = lax.map(
        lambda packed: head_pass(*packed, offset),
        (per_query, cache_k, cache_v, fresh_k, fresh_v, per_grad),
    )
    attended = results[0].transpose(2, 0, 1, 3).reshape(tokens_dev, kv_local * group * HD)
    grad_query = results[1].transpose(2, 0, 1, 3).reshape(tokens_dev, kv_local * group * HD)
    grad_keys = results[2].transpose(1, 0, 2).reshape(tokens_dev, kv_local * HD)
    grad_values = results[3].transpose(1, 0, 2).reshape(tokens_dev, kv_local * HD)
    grads_cat = jnp.concatenate([grad_query, grad_keys, grad_values], 1)
    tp_count = lax.axis_size("tp")
    z_count = lax.axis_size("z")
    rows = w_query.shape[0]
    chip_core = lax.axis_index("c")
    x_pos = lax.axis_index("xl")
    by_place = hidden_in.reshape(tokens_dev, 2, z_count, 2, rows).transpose(0, 2, 1, 3, 4)
    cols_other = lax.dynamic_index_in_dim(by_place, 1 - chip_core, 3, False)
    cols_own = lax.dynamic_index_in_dim(by_place, chip_core, 3, False)
    part_other = contract_first(cols_other.reshape(tokens_dev, -1), grads_cat)
    from_peer = lax.ppermute(part_other, "c", SWAP)
    part_own = contract_first(cols_own.reshape(tokens_dev, -1), grads_cat)
    chip_sum = (part_own + from_peer).astype(jnp.bfloat16)
    ring_sum = lax.psum_scatter(chip_sum, "z", scatter_dimension=0, tiled=True)
    ring_sum = ring_sum.reshape(2, rows, -1)
    keep = lax.dynamic_index_in_dim(ring_sum, x_pos, 0, False)
    give = lax.dynamic_index_in_dim(ring_sum, 1 - x_pos, 0, False)
    summed = keep.astype(jnp.float32) + lax.ppermute(give, "xl", SWAP).astype(jnp.float32)
    input_term = contract_last(grads_cat, full_w).astype(jnp.bfloat16)
    input_term = input_term.reshape(tokens_dev, tp_count, -1).transpose(1, 0, 2)
    gathered = lax.all_to_all(input_term, "tp", 0, 0, tiled=True)
    grad_in = jnp.sum(gathered.astype(jnp.float32), axis=0).astype(jnp.bfloat16)
    summed = summed * (tokens_dev * lax.axis_size(BLK)) ** (-0.5)
    grad_wq = summed[:, :query_cols]
    grad_wk = summed[:, query_cols : query_cols + kv_cols]
    grad_wv = summed[:, query_cols + kv_cols :]
    return (attended, grad_in, grad_wq, grad_wk, grad_wv)


def solution(mesh):
    blk = mesh.shape["blk"]
    devices = mesh.devices.reshape(2, blk // 4, 2, mesh.shape["tp"])
    split = Mesh(devices, BLK + ("tp",))
    in_specs = (
        P(BLK, None),
        P(BLK, "tp"),
        P(BLK, "tp"),
        P(BLK, "tp"),
        P(BLK),
        P(BLK, None, "tp"),
        P(BLK, None, "tp"),
        P(BLK, "tp"),
    )
    out_specs = (P(BLK, "tp"),) * 5
    return jax.shard_map(local, mesh=split, in_specs=in_specs, out_specs=out_specs, check_vma=False)
```

```python
import jax
import jax.numpy as jnp
from jax import lax
from jax.sharding import Mesh, PartitionSpec as P

H = 32
KV = 8
HD = 128
SWAP = [(0, 1), (1, 0)]
BLK = ("xl", "z", "c")


def contract_last(left, right):
    return lax.dot_general(
        left, right, (((1,), (1,)), ((), ())), preferred_element_type=jnp.float32
    )


def contract_first(left, right):
    return lax.dot_general(
        left, right, (((0,), (0,)), ((), ())), preferred_element_type=jnp.float32
    )


def head_pass(queries, cache_keys, cache_values, fresh_keys, fresh_values, grad_heads, offset):
    groups, row_count, head_width = queries.shape
    cached = cache_keys.shape[0]
    factor = head_width ** (-0.5)
    key_list = jnp.concatenate([cache_keys, fresh_keys], 0)
    value_list = jnp.concatenate([cache_values, fresh_values], 0)
    flat_query = queries.reshape(groups * row_count, head_width)
    flat_grad = grad_heads.reshape(groups * row_count, head_width)
    scores = contract_last(flat_query, key_list) * factor
    scores = scores.reshape(groups, row_count, cached + row_count)
    row_pos = lax.iota(jnp.int32, row_count)
    cache_ok = jnp.broadcast_to(lax.iota(jnp.int32, cached)[None, :] < offset, (row_count, cached))
    own_ok = row_pos[None, :] <= row_pos[:, None]
    allowed = jnp.concatenate([cache_ok, own_ok], 1)
    scores = jnp.where(allowed[None], scores, -jnp.inf)
    row_max = jnp.max(scores, axis=-1, keepdims=True)
    expo = jnp.exp(scores - row_max)
    probs = (expo / jnp.sum(expo, axis=-1, keepdims=True)).astype(jnp.bfloat16)
    probs = probs.reshape(groups * row_count, cached + row_count)
    attended = jnp.dot(probs, value_list, preferred_element_type=jnp.float32).astype(jnp.bfloat16)
    grad_probs = contract_last(flat_grad, value_list)
    probs_wide = probs.astype(jnp.float32)
    row_dot = jnp.sum(probs_wide * grad_probs, axis=-1, keepdims=True)
    grad_scores = (probs_wide * (grad_probs - row_dot) * factor).astype(jnp.bfloat16)
    grad_query = jnp.dot(grad_scores, key_list, preferred_element_type=jnp.float32).astype(
        jnp.bfloat16
    )
    grad_keys = contract_first(grad_scores[:, cached:], flat_query).astype(jnp.bfloat16)
    grad_values = contract_first(probs[:, cached:], flat_grad).astype(jnp.bfloat16)
    return (
        attended.reshape(groups, row_count, head_width),
        grad_query.reshape(groups, row_count, head_width),
        grad_keys,
        grad_values,
    )


def gather_rows(block):
    rows, width = block.shape
    z_count = lax.axis_size("z")
    x_pos = lax.axis_index("xl")
    z_pos = lax.axis_index("z")
    chip_core = lax.axis_index("c")
    peer = lax.ppermute(block, "xl", SWAP)
    pair = jnp.stack([jnp.where(x_pos == 0, block, peer), jnp.where(x_pos == 0, peer, block)])
    ahead = [(i, (i + 1) % z_count) for i in range(z_count)]
    behind = [(i, (i - 1) % z_count) for i in range(z_count)]
    ring = jnp.zeros((z_count,) + pair.shape, pair.dtype)
    ring = lax.dynamic_update_index_in_dim(ring, pair, z_pos, 0)
    fwd = pair
    bwd = pair
    for step in range(1, z_count // 2 + 1):
        fwd = lax.ppermute(fwd, "z", ahead)
        ring = lax.dynamic_update_index_in_dim(ring, fwd, (z_pos - step) % z_count, 0)
        if step < z_count - z_count // 2:
            bwd = lax.ppermute(bwd, "z", behind)
            ring = lax.dynamic_update_index_in_dim(ring, bwd, (z_pos + step) % z_count, 0)
    other = lax.ppermute(ring, "c", SWAP)
    first = jnp.where(chip_core == 0, ring, other)
    second = jnp.where(chip_core == 0, other, ring)
    full = jnp.stack([first, second], 2)
    return full.transpose(1, 0, 2, 3, 4).reshape(-1, width)


def local(hidden_in, w_query, w_key, w_value, starts, key_cache, value_cache, grad_out):
    tokens_dev = hidden_in.shape[0]
    kv_local = w_key.shape[1] // HD
    group = H // KV
    cached = key_cache.shape[1]
    query_cols = w_query.shape[1]
    kv_cols = w_key.shape[1]
    local_w = jnp.concatenate([w_query, w_key, w_value], 1)
    full_w = gather_rows(local_w)
    proj = jnp.dot(hidden_in, full_w, preferred_element_type=jnp.float32)
    queries = proj[:, :query_cols].astype(jnp.bfloat16)
    new_keys = proj[:, query_cols : query_cols + kv_cols].astype(jnp.bfloat16)
    new_values = proj[:, query_cols + kv_cols :].astype(jnp.bfloat16)
    per_query = queries.reshape(tokens_dev, kv_local, group, HD).transpose(1, 2, 0, 3)
    per_grad = grad_out.reshape(tokens_dev, kv_local, group, HD).transpose(1, 2, 0, 3)
    cache_k = key_cache[0].reshape(cached, kv_local, HD).transpose(1, 0, 2)
    cache_v = value_cache[0].reshape(cached, kv_local, HD).transpose(1, 0, 2)
    fresh_k = new_keys.reshape(tokens_dev, kv_local, HD).transpose(1, 0, 2)
    fresh_v = new_values.reshape(tokens_dev, kv_local, HD).transpose(1, 0, 2)
    offset = starts[0]
    results = lax.map(
        lambda packed: head_pass(*packed, offset),
        (per_query, cache_k, cache_v, fresh_k, fresh_v, per_grad),
    )
    attended = results[0].transpose(2, 0, 1, 3).reshape(tokens_dev, kv_local * group * HD)
    grad_query = results[1].transpose(2, 0, 1, 3).reshape(tokens_dev, kv_local * group * HD)
    grad_keys = results[2].transpose(1, 0, 2).reshape(tokens_dev, kv_local * HD)
    grad_values = results[3].transpose(1, 0, 2).reshape(tokens_dev, kv_local * HD)
    grads_cat = jnp.concatenate([grad_query, grad_keys, grad_values], 1)
    tp_count = lax.axis_size("tp")
    z_count = lax.axis_size("z")
    rows = w_query.shape[0]
    chip_core = lax.axis_index("c")
    x_pos = lax.axis_index("xl")
    by_place = hidden_in.reshape(tokens_dev, 2, z_count, 2, rows).transpose(0, 2, 1, 3, 4)
    cols_other = lax.dynamic_index_in_dim(by_place, 1 - chip_core, 3, False)
    cols_own = lax.dynamic_index_in_dim(by_place, chip_core, 3, False)
    part_other = contract_first(cols_other.reshape(tokens_dev, -1), grads_cat)
    from_peer = lax.ppermute(part_other, "c", SWAP)
    part_own = contract_first(cols_own.reshape(tokens_dev, -1), grads_cat)
    chip_sum = (part_own + from_peer).astype(jnp.bfloat16)
    ring_sum = lax.psum_scatter(chip_sum, "z", scatter_dimension=0, tiled=True)
    ring_sum = ring_sum.reshape(2, rows, -1)
    keep = lax.dynamic_index_in_dim(ring_sum, x_pos, 0, False)
    give = lax.dynamic_index_in_dim(ring_sum, 1 - x_pos, 0, False)
    summed = keep.astype(jnp.float32) + lax.ppermute(give, "xl", SWAP).astype(jnp.float32)
    input_term = contract_last(grads_cat, full_w).astype(jnp.bfloat16)
    input_term = input_term.reshape(tokens_dev, tp_count, -1).transpose(1, 0, 2)
    gathered = lax.all_to_all(input_term, "tp", 0, 0, tiled=True)
    grad_in = jnp.sum(gathered.astype(jnp.float32), axis=0).astype(jnp.bfloat16)
    summed = summed * (tokens_dev * lax.axis_size(BLK)) ** (-0.5)
    grad_wq = summed[:, :query_cols]
    grad_wk = summed[:, query_cols : query_cols + kv_cols]
    grad_wv = summed[:, query_cols + kv_cols :]
    return (attended, grad_in, grad_wq, grad_wk, grad_wv)


def solution(mesh):
    blk = mesh.shape["blk"]
    devices = mesh.devices.reshape(2, blk // 4, 2, mesh.shape["tp"])
    split = Mesh(devices, BLK + ("tp",))
    in_specs = (
        P(BLK, None),
        P(BLK, "tp"),
        P(BLK, "tp"),
        P(BLK, "tp"),
        P(BLK),
        P(BLK, None, "tp"),
        P(BLK, None, "tp"),
        P(BLK, "tp"),
    )
    out_specs = (P(BLK, "tp"),) * 5
    return jax.shard_map(local, mesh=split, in_specs=in_specs, out_specs=out_specs, check_vma=False)
```

```python
import jax
import jax.numpy as jnp
from jax import lax
from jax.sharding import Mesh, PartitionSpec as P

H = 32
KV = 8
HD = 128
SWAP = [(0, 1), (1, 0)]
BLK = ("xl", "z", "c")


def contract_last(left, right):
    return lax.dot_general(
        left, right, (((1,), (1,)), ((), ())), preferred_element_type=jnp.float32
    )


def contract_first(left, right):
    return lax.dot_general(
        left, right, (((0,), (0,)), ((), ())), preferred_element_type=jnp.float32
    )


def head_pass(queries, cache_keys, cache_values, fresh_keys, fresh_values, grad_heads, offset):
    groups, row_count, head_width = queries.shape
    cached = cache_keys.shape[0]
    factor = head_width ** (-0.5)
    key_list = jnp.concatenate([cache_keys, fresh_keys], 0)
    value_list = jnp.concatenate([cache_values, fresh_values], 0)
    flat_query = queries.reshape(groups * row_count, head_width)
    flat_grad = grad_heads.reshape(groups * row_count, head_width)
    scores = contract_last(flat_query, key_list) * factor
    scores = scores.reshape(groups, row_count, cached + row_count)
    row_pos = lax.iota(jnp.int32, row_count)
    cache_ok = jnp.broadcast_to(lax.iota(jnp.int32, cached)[None, :] < offset, (row_count, cached))
    own_ok = row_pos[None, :] <= row_pos[:, None]
    allowed = jnp.concatenate([cache_ok, own_ok], 1)
    scores = jnp.where(allowed[None], scores, -jnp.inf)
    row_max = jnp.max(scores, axis=-1, keepdims=True)
    expo = jnp.exp(scores - row_max)
    probs = (expo / jnp.sum(expo, axis=-1, keepdims=True)).astype(jnp.bfloat16)
    probs = probs.reshape(groups * row_count, cached + row_count)
    attended = jnp.dot(probs, value_list, preferred_element_type=jnp.float32).astype(jnp.bfloat16)
    grad_probs = contract_last(flat_grad, value_list)
    probs_wide = probs.astype(jnp.float32)
    row_dot = jnp.sum(probs_wide * grad_probs, axis=-1, keepdims=True)
    grad_scores = (probs_wide * (grad_probs - row_dot) * factor).astype(jnp.bfloat16)
    grad_query = jnp.dot(grad_scores, key_list, preferred_element_type=jnp.float32).astype(
        jnp.bfloat16
    )
    grad_keys = contract_first(grad_scores[:, cached:], flat_query).astype(jnp.bfloat16)
    grad_values = contract_first(probs[:, cached:], flat_grad).astype(jnp.bfloat16)
    return (
        attended.reshape(groups, row_count, head_width),
        grad_query.reshape(groups, row_count, head_width),
        grad_keys,
        grad_values,
    )


def gather_rows(block):
    rows, width = block.shape
    z_count = lax.axis_size("z")
    x_pos = lax.axis_index("xl")
    z_pos = lax.axis_index("z")
    chip_core = lax.axis_index("c")
    peer = lax.ppermute(block, "xl", SWAP)
    pair = jnp.stack([jnp.where(x_pos == 0, block, peer), jnp.where(x_pos == 0, peer, block)])
    ahead = [(i, (i + 1) % z_count) for i in range(z_count)]
    behind = [(i, (i - 1) % z_count) for i in range(z_count)]
    got = [(pair, z_pos)]
    fwd = pair
    bwd = pair
    for step in range(1, z_count // 2 + 1):
        fwd = lax.ppermute(fwd, "z", ahead)
        got.append((fwd, (z_pos - step) % z_count))
        if step < z_count - z_count // 2:
            bwd = lax.ppermute(bwd, "z", behind)
            got.append((bwd, (z_pos + step) % z_count))
    full = jnp.zeros((2, z_count, 2, rows, width), block.dtype)
    early = len(got) // 2 + 1
    for lo, hi in ((0, early), (early, len(got))):
        mine = jnp.stack([chunk for chunk, _ in got[lo:hi]])
        theirs = lax.ppermute(mine, "c", SWAP)
        for k in range(hi - lo):
            place = got[lo + k][1]
            full = lax.dynamic_update_slice(full, mine[k][:, None, None], (0, place, chip_core, 0, 0))
            full = lax.dynamic_update_slice(full, theirs[k][:, None, None], (0, place, 1 - chip_core, 0, 0))
    return full.reshape(-1, width)


def local(hidden_in, w_query, w_key, w_value, starts, key_cache, value_cache, grad_out):
    tokens_dev = hidden_in.shape[0]
    kv_local = w_key.shape[1] // HD
    group = H // KV
    cached = key_cache.shape[1]
    query_cols = w_query.shape[1]
    kv_cols = w_key.shape[1]
    local_w = jnp.concatenate([w_query, w_key, w_value], 1)
    full_w = gather_rows(local_w)
    proj = jnp.dot(hidden_in, full_w, preferred_element_type=jnp.float32)
    queries = proj[:, :query_cols].astype(jnp.bfloat16)
    new_keys = proj[:, query_cols : query_cols + kv_cols].astype(jnp.bfloat16)
    new_values = proj[:, query_cols + kv_cols :].astype(jnp.bfloat16)
    per_query = queries.reshape(tokens_dev, kv_local, group, HD).transpose(1, 2, 0, 3)
    per_grad = grad_out.reshape(tokens_dev, kv_local, group, HD).transpose(1, 2, 0, 3)
    cache_k = key_cache[0].reshape(cached, kv_local, HD).transpose(1, 0, 2)
    cache_v = value_cache[0].reshape(cached, kv_local, HD).transpose(1, 0, 2)
    fresh_k = new_keys.reshape(tokens_dev, kv_local, HD).transpose(1, 0, 2)
    fresh_v = new_values.reshape(tokens_dev, kv_local, HD).transpose(1, 0, 2)
    offset = starts[0]
    results = lax.map(
        lambda packed: head_pass(*packed, offset),
        (per_query, cache_k, cache_v, fresh_k, fresh_v, per_grad),
    )
    attended = results[0].transpose(2, 0, 1, 3).reshape(tokens_dev, kv_local * group * HD)
    grad_query = results[1].transpose(2, 0, 1, 3).reshape(tokens_dev, kv_local * group * HD)
    grad_keys = results[2].transpose(1, 0, 2).reshape(tokens_dev, kv_local * HD)
    grad_values = results[3].transpose(1, 0, 2).reshape(tokens_dev, kv_local * HD)
    grads_cat = jnp.concatenate([grad_query, grad_keys, grad_values], 1)
    tp_count = lax.axis_size("tp")
    z_count = lax.axis_size("z")
    rows = w_query.shape[0]
    chip_core = lax.axis_index("c")
    x_pos = lax.axis_index("xl")
    by_place = hidden_in.reshape(tokens_dev, 2, z_count, 2, rows).transpose(0, 2, 1, 3, 4)
    cols_other = lax.dynamic_index_in_dim(by_place, 1 - chip_core, 3, False)
    cols_own = lax.dynamic_index_in_dim(by_place, chip_core, 3, False)
    part_other = contract_first(cols_other.reshape(tokens_dev, -1), grads_cat)
    from_peer = lax.ppermute(part_other.astype(jnp.bfloat16), "c", SWAP)
    part_own = contract_first(cols_own.reshape(tokens_dev, -1), grads_cat)
    chip_sum = (part_own + from_peer.astype(jnp.float32)).astype(jnp.bfloat16)
    ring_sum = lax.psum_scatter(chip_sum, "z", scatter_dimension=0, tiled=True)
    ring_sum = ring_sum.reshape(2, rows, -1)
    keep = lax.dynamic_index_in_dim(ring_sum, x_pos, 0, False)
    give = lax.dynamic_index_in_dim(ring_sum, 1 - x_pos, 0, False)
    summed = keep.astype(jnp.float32) + lax.ppermute(give, "xl", SWAP).astype(jnp.float32)
    input_term = contract_last(grads_cat, full_w).astype(jnp.bfloat16)
    input_term = input_term.reshape(tokens_dev, tp_count, -1).transpose(1, 0, 2)
    gathered = lax.all_to_all(input_term, "tp", 0, 0, tiled=True)
    grad_in = jnp.sum(gathered.astype(jnp.float32), axis=0).astype(jnp.bfloat16)
    summed = summed * (tokens_dev * lax.axis_size(BLK)) ** (-0.5)
    grad_wq = summed[:, :query_cols]
    grad_wk = summed[:, query_cols : query_cols + kv_cols]
    grad_wv = summed[:, query_cols + kv_cols :]
    return (attended, grad_in, grad_wq, grad_wk, grad_wv)


def solution(mesh):
    blk = mesh.shape["blk"]
    devices = mesh.devices.reshape(2, blk // 4, 2, mesh.shape["tp"])
    split = Mesh(devices, BLK + ("tp",))
    in_specs = (
        P(BLK, None),
        P(BLK, "tp"),
        P(BLK, "tp"),
        P(BLK, "tp"),
        P(BLK),
        P(BLK, None, "tp"),
        P(BLK, None, "tp"),
        P(BLK, "tp"),
    )
    out_specs = (P(BLK, "tp"),) * 5
    return jax.shard_map(local, mesh=split, in_specs=in_specs, out_specs=out_specs, check_vma=False)
```

```python
import jax
import jax.numpy as jnp
from jax import lax
from jax.sharding import Mesh, PartitionSpec as P

H = 32
KV = 8
HD = 128
SWAP = [(0, 1), (1, 0)]
BLK = ("xl", "z", "c")


def contract_last(left, right):
    return lax.dot_general(
        left, right, (((1,), (1,)), ((), ())), preferred_element_type=jnp.float32
    )


def contract_first(left, right):
    return lax.dot_general(
        left, right, (((0,), (0,)), ((), ())), preferred_element_type=jnp.float32
    )


def head_pass(queries, cache_keys, cache_values, fresh_keys, fresh_values, grad_heads, offset):
    groups, row_count, head_width = queries.shape
    cached = cache_keys.shape[0]
    factor = head_width ** (-0.5)
    key_list = jnp.concatenate([cache_keys, fresh_keys], 0)
    value_list = jnp.concatenate([cache_values, fresh_values], 0)
    flat_query = queries.reshape(groups * row_count, head_width)
    flat_grad = grad_heads.reshape(groups * row_count, head_width)
    scores = contract_last(flat_query, key_list) * factor
    scores = scores.reshape(groups, row_count, cached + row_count)
    row_pos = lax.iota(jnp.int32, row_count)
    cache_ok = jnp.broadcast_to(lax.iota(jnp.int32, cached)[None, :] < offset, (row_count, cached))
    own_ok = row_pos[None, :] <= row_pos[:, None]
    allowed = jnp.concatenate([cache_ok, own_ok], 1)
    scores = jnp.where(allowed[None], scores, -jnp.inf)
    row_max = jnp.max(scores, axis=-1, keepdims=True)
    expo = jnp.exp(scores - row_max)
    probs = (expo / jnp.sum(expo, axis=-1, keepdims=True)).astype(jnp.bfloat16)
    probs = probs.reshape(groups * row_count, cached + row_count)
    attended = jnp.dot(probs, value_list, preferred_element_type=jnp.float32).astype(jnp.bfloat16)
    grad_probs = contract_last(flat_grad, value_list)
    probs_wide = probs.astype(jnp.float32)
    row_dot = jnp.sum(probs_wide * grad_probs, axis=-1, keepdims=True)
    grad_scores = (probs_wide * (grad_probs - row_dot) * factor).astype(jnp.bfloat16)
    grad_query = jnp.dot(grad_scores, key_list, preferred_element_type=jnp.float32).astype(
        jnp.bfloat16
    )
    grad_keys = contract_first(grad_scores[:, cached:], flat_query).astype(jnp.bfloat16)
    grad_values = contract_first(probs[:, cached:], flat_grad).astype(jnp.bfloat16)
    return (
        attended.reshape(groups, row_count, head_width),
        grad_query.reshape(groups, row_count, head_width),
        grad_keys,
        grad_values,
    )


def gather_rows(block):
    rows, width = block.shape
    z_count = lax.axis_size("z")
    x_pos = lax.axis_index("xl")
    z_pos = lax.axis_index("z")
    chip_core = lax.axis_index("c")
    peer = lax.ppermute(block, "xl", SWAP)
    pair = jnp.stack([jnp.where(x_pos == 0, block, peer), jnp.where(x_pos == 0, peer, block)])
    ahead = [(i, (i + 1) % z_count) for i in range(z_count)]
    behind = [(i, (i - 1) % z_count) for i in range(z_count)]
    ring = jnp.zeros((z_count,) + pair.shape, pair.dtype)
    ring = lax.dynamic_update_index_in_dim(ring, pair, z_pos, 0)
    fwd = pair
    bwd = pair
    for step in range(1, z_count // 2 + 1):
        fwd = lax.ppermute(fwd, "z", ahead)
        ring = lax.dynamic_update_index_in_dim(ring, fwd, (z_pos - step) % z_count, 0)
        if step < z_count - z_count // 2:
            bwd = lax.ppermute(bwd, "z", behind)
            ring = lax.dynamic_update_index_in_dim(ring, bwd, (z_pos + step) % z_count, 0)
    other = lax.ppermute(ring, "c", SWAP)
    first = jnp.where(chip_core == 0, ring, other)
    second = jnp.where(chip_core == 0, other, ring)
    full = jnp.stack([first, second], 2)
    return full.transpose(1, 0, 2, 3, 4).reshape(-1, width)


def local(hidden_in, w_query, w_key, w_value, starts, key_cache, value_cache, grad_out):
    tokens_dev = hidden_in.shape[0]
    kv_local = w_key.shape[1] // HD
    group = H // KV
    cached = key_cache.shape[1]
    query_cols = w_query.shape[1]
    kv_cols = w_key.shape[1]
    local_w = jnp.concatenate([w_query, w_key, w_value], 1)
    full_w = gather_rows(local_w)
    proj = jnp.dot(hidden_in, full_w, preferred_element_type=jnp.float32)
    queries = proj[:, :query_cols].astype(jnp.bfloat16)
    new_keys = proj[:, query_cols : query_cols + kv_cols].astype(jnp.bfloat16)
    new_values = proj[:, query_cols + kv_cols :].astype(jnp.bfloat16)
    per_query = queries.reshape(tokens_dev, kv_local, group, HD).transpose(1, 2, 0, 3)
    per_grad = grad_out.reshape(tokens_dev, kv_local, group, HD).transpose(1, 2, 0, 3)
    cache_k = key_cache[0].reshape(cached, kv_local, HD).transpose(1, 0, 2)
    cache_v = value_cache[0].reshape(cached, kv_local, HD).transpose(1, 0, 2)
    fresh_k = new_keys.reshape(tokens_dev, kv_local, HD).transpose(1, 0, 2)
    fresh_v = new_values.reshape(tokens_dev, kv_local, HD).transpose(1, 0, 2)
    offset = starts[0]
    results = lax.map(
        lambda packed: head_pass(*packed, offset),
        (per_query, cache_k, cache_v, fresh_k, fresh_v, per_grad),
    )
    attended = results[0].transpose(2, 0, 1, 3).reshape(tokens_dev, kv_local * group * HD)
    grad_query = results[1].transpose(2, 0, 1, 3).reshape(tokens_dev, kv_local * group * HD)
    grad_keys = results[2].transpose(1, 0, 2).reshape(tokens_dev, kv_local * HD)
    grad_values = results[3].transpose(1, 0, 2).reshape(tokens_dev, kv_local * HD)
    grads_cat = jnp.concatenate([grad_query, grad_keys, grad_values], 1)
    tp_count = lax.axis_size("tp")
    z_count = lax.axis_size("z")
    rows = w_query.shape[0]
    chip_core = lax.axis_index("c")
    x_pos = lax.axis_index("xl")
    by_place = hidden_in.reshape(tokens_dev, 2, z_count, 2, rows).transpose(0, 2, 1, 3, 4)
    cols_other = lax.dynamic_index_in_dim(by_place, 1 - chip_core, 3, False)
    cols_own = lax.dynamic_index_in_dim(by_place, chip_core, 3, False)
    part_other = contract_first(cols_other.reshape(tokens_dev, -1), grads_cat)
    from_peer = lax.ppermute(part_other.astype(jnp.bfloat16), "c", SWAP)
    part_own = contract_first(cols_own.reshape(tokens_dev, -1), grads_cat)
    chip_sum = (part_own + from_peer.astype(jnp.float32)).astype(jnp.bfloat16)
    ring_sum = lax.psum_scatter(chip_sum, "z", scatter_dimension=0, tiled=True)
    ring_sum = ring_sum.reshape(2, rows, -1)
    keep = lax.dynamic_index_in_dim(ring_sum, x_pos, 0, False)
    give = lax.dynamic_index_in_dim(ring_sum, 1 - x_pos, 0, False)
    summed = keep.astype(jnp.float32) + lax.ppermute(give, "xl", SWAP).astype(jnp.float32)
    input_term = contract_last(grads_cat, full_w).astype(jnp.bfloat16)
    input_term = input_term.reshape(tokens_dev, tp_count, -1).transpose(1, 0, 2)
    gathered = lax.all_to_all(input_term, "tp", 0, 0, tiled=True)
    grad_in = jnp.sum(gathered.astype(jnp.float32), axis=0).astype(jnp.bfloat16)
    summed = summed * (tokens_dev * lax.axis_size(BLK)) ** (-0.5)
    grad_wq = summed[:, :query_cols]
    grad_wk = summed[:, query_cols : query_cols + kv_cols]
    grad_wv = summed[:, query_cols + kv_cols :]
    return (attended, grad_in, grad_wq, grad_wk, grad_wv)


def solution(mesh):
    blk = mesh.shape["blk"]
    devices = mesh.devices.reshape(2, blk // 4, 2, mesh.shape["tp"])
    split = Mesh(devices, BLK + ("tp",))
    in_specs = (
        P(BLK, None),
        P(BLK, "tp"),
        P(BLK, "tp"),
        P(BLK, "tp"),
        P(BLK),
        P(BLK, None, "tp"),
        P(BLK, None, "tp"),
        P(BLK, "tp"),
    )
    out_specs = (P(BLK, "tp"),) * 5
    return jax.shard_map(local, mesh=split, in_specs=in_specs, out_specs=out_specs, check_vma=False)
```

```python
import jax
import jax.numpy as jnp
from jax import lax
from jax.sharding import Mesh, PartitionSpec as P

H = 32
KV = 8
HD = 128
SWAP = [(0, 1), (1, 0)]
BLK = ("xl", "z", "c")


def contract_last(left, right):
    return lax.dot_general(
        left, right, (((1,), (1,)), ((), ())), preferred_element_type=jnp.float32
    )


def contract_first(left, right):
    return lax.dot_general(
        left, right, (((0,), (0,)), ((), ())), preferred_element_type=jnp.float32
    )


def head_pass(queries, cache_keys, cache_values, fresh_keys, fresh_values, grad_heads, offset):
    groups, row_count, head_width = queries.shape
    cached = cache_keys.shape[0]
    factor = head_width ** (-0.5)
    key_list = jnp.concatenate([cache_keys, fresh_keys], 0)
    value_list = jnp.concatenate([cache_values, fresh_values], 0)
    flat_query = queries.reshape(groups * row_count, head_width)
    flat_grad = grad_heads.reshape(groups * row_count, head_width)
    scores = contract_last(flat_query, key_list) * factor
    scores = scores.reshape(groups, row_count, cached + row_count)
    row_pos = lax.iota(jnp.int32, row_count)
    cache_ok = jnp.broadcast_to(lax.iota(jnp.int32, cached)[None, :] < offset, (row_count, cached))
    own_ok = row_pos[None, :] <= row_pos[:, None]
    allowed = jnp.concatenate([cache_ok, own_ok], 1)
    scores = jnp.where(allowed[None], scores, -jnp.inf)
    row_max = jnp.max(scores, axis=-1, keepdims=True)
    expo = jnp.exp(scores - row_max)
    probs = (expo / jnp.sum(expo, axis=-1, keepdims=True)).astype(jnp.bfloat16)
    probs = probs.reshape(groups * row_count, cached + row_count)
    attended = jnp.dot(probs, value_list, preferred_element_type=jnp.float32).astype(jnp.bfloat16)
    grad_probs = contract_last(flat_grad, value_list)
    probs_wide = probs.astype(jnp.float32)
    row_dot = jnp.sum(probs_wide * grad_probs, axis=-1, keepdims=True)
    grad_scores = (probs_wide * (grad_probs - row_dot) * factor).astype(jnp.bfloat16)
    grad_query = jnp.dot(grad_scores, key_list, preferred_element_type=jnp.float32).astype(
        jnp.bfloat16
    )
    grad_keys = contract_first(grad_scores[:, cached:], flat_query).astype(jnp.bfloat16)
    grad_values = contract_first(probs[:, cached:], flat_grad).astype(jnp.bfloat16)
    return (
        attended.reshape(groups, row_count, head_width),
        grad_query.reshape(groups, row_count, head_width),
        grad_keys,
        grad_values,
    )


def gather_rows(block):
    rows, width = block.shape
    z_count = lax.axis_size("z")
    x_pos = lax.axis_index("xl")
    z_pos = lax.axis_index("z")
    chip_core = lax.axis_index("c")
    peer = lax.ppermute(block, "xl", SWAP)
    pair = jnp.stack([jnp.where(x_pos == 0, block, peer), jnp.where(x_pos == 0, peer, block)])
    ahead = [(i, (i + 1) % z_count) for i in range(z_count)]
    behind = [(i, (i - 1) % z_count) for i in range(z_count)]
    ring = jnp.zeros((z_count,) + pair.shape, pair.dtype)
    ring = lax.dynamic_update_index_in_dim(ring, pair, z_pos, 0)
    half = z_count // 2

    def ring_step(step, carry):
        ring, fwd, bwd = carry
        fwd = lax.ppermute(fwd, "z", ahead)
        bwd = lax.ppermute(bwd, "z", behind)
        ring = lax.dynamic_update_index_in_dim(ring, fwd, (z_pos - step) % z_count, 0)
        ring = lax.dynamic_update_index_in_dim(ring, bwd, (z_pos + step) % z_count, 0)
        return ring, fwd, bwd

    ring, _, _ = lax.fori_loop(1, half + 1, ring_step, (ring, pair, pair))
    other = lax.ppermute(ring, "c", SWAP)
    first = jnp.where(chip_core == 0, ring, other)
    second = jnp.where(chip_core == 0, other, ring)
    full = jnp.stack([first, second], 2)
    return full.transpose(1, 0, 2, 3, 4).reshape(-1, width)


def local(hidden_in, w_query, w_key, w_value, starts, key_cache, value_cache, grad_out):
    tokens_dev = hidden_in.shape[0]
    kv_local = w_key.shape[1] // HD
    group = H // KV
    cached = key_cache.shape[1]
    query_cols = w_query.shape[1]
    kv_cols = w_key.shape[1]
    local_w = jnp.concatenate([w_query, w_key, w_value], 1)
    full_w = gather_rows(local_w)
    proj = jnp.dot(hidden_in, full_w, preferred_element_type=jnp.float32)
    queries = proj[:, :query_cols].astype(jnp.bfloat16)
    new_keys = proj[:, query_cols : query_cols + kv_cols].astype(jnp.bfloat16)
    new_values = proj[:, query_cols + kv_cols :].astype(jnp.bfloat16)
    per_query = queries.reshape(tokens_dev, kv_local, group, HD).transpose(1, 2, 0, 3)
    per_grad = grad_out.reshape(tokens_dev, kv_local, group, HD).transpose(1, 2, 0, 3)
    cache_k = key_cache[0].reshape(cached, kv_local, HD).transpose(1, 0, 2)
    cache_v = value_cache[0].reshape(cached, kv_local, HD).transpose(1, 0, 2)
    fresh_k = new_keys.reshape(tokens_dev, kv_local, HD).transpose(1, 0, 2)
    fresh_v = new_values.reshape(tokens_dev, kv_local, HD).transpose(1, 0, 2)
    offset = starts[0]
    results = lax.map(
        lambda packed: head_pass(*packed, offset),
        (per_query, cache_k, cache_v, fresh_k, fresh_v, per_grad),
    )
    attended = results[0].transpose(2, 0, 1, 3).reshape(tokens_dev, kv_local * group * HD)
    grad_query = results[1].transpose(2, 0, 1, 3).reshape(tokens_dev, kv_local * group * HD)
    grad_keys = results[2].transpose(1, 0, 2).reshape(tokens_dev, kv_local * HD)
    grad_values = results[3].transpose(1, 0, 2).reshape(tokens_dev, kv_local * HD)
    grads_cat = jnp.concatenate([grad_query, grad_keys, grad_values], 1)
    tp_count = lax.axis_size("tp")
    z_count = lax.axis_size("z")
    rows = w_query.shape[0]
    chip_core = lax.axis_index("c")
    x_pos = lax.axis_index("xl")
    by_place = hidden_in.reshape(tokens_dev, 2, z_count, 2, rows).transpose(0, 2, 1, 3, 4)
    cols_other = lax.dynamic_index_in_dim(by_place, 1 - chip_core, 3, False)
    cols_own = lax.dynamic_index_in_dim(by_place, chip_core, 3, False)
    part_other = contract_first(cols_other.reshape(tokens_dev, -1), grads_cat)
    from_peer = lax.ppermute(part_other.astype(jnp.bfloat16), "c", SWAP)
    part_own = contract_first(cols_own.reshape(tokens_dev, -1), grads_cat)
    chip_sum = (part_own + from_peer.astype(jnp.float32)).astype(jnp.bfloat16)
    ring_sum = lax.psum_scatter(chip_sum, "z", scatter_dimension=0, tiled=True)
    ring_sum = ring_sum.reshape(2, rows, -1)
    keep = lax.dynamic_index_in_dim(ring_sum, x_pos, 0, False)
    give = lax.dynamic_index_in_dim(ring_sum, 1 - x_pos, 0, False)
    summed = keep.astype(jnp.float32) + lax.ppermute(give, "xl", SWAP).astype(jnp.float32)
    input_term = contract_last(grads_cat, full_w).astype(jnp.bfloat16)
    input_term = input_term.reshape(tokens_dev, tp_count, -1).transpose(1, 0, 2)
    gathered = lax.all_to_all(input_term, "tp", 0, 0, tiled=True)
    grad_in = jnp.sum(gathered.astype(jnp.float32), axis=0).astype(jnp.bfloat16)
    summed = summed * (tokens_dev * lax.axis_size(BLK)) ** (-0.5)
    grad_wq = summed[:, :query_cols]
    grad_wk = summed[:, query_cols : query_cols + kv_cols]
    grad_wv = summed[:, query_cols + kv_cols :]
    return (attended, grad_in, grad_wq, grad_wk, grad_wv)


def solution(mesh):
    blk = mesh.shape["blk"]
    devices = mesh.devices.reshape(2, blk // 4, 2, mesh.shape["tp"])
    split = Mesh(devices, BLK + ("tp",))
    in_specs = (
        P(BLK, None),
        P(BLK, "tp"),
        P(BLK, "tp"),
        P(BLK, "tp"),
        P(BLK),
        P(BLK, None, "tp"),
        P(BLK, None, "tp"),
        P(BLK, "tp"),
    )
    out_specs = (P(BLK, "tp"),) * 5
    return jax.shard_map(local, mesh=split, in_specs=in_specs, out_specs=out_specs, check_vma=False)
```

```python
import jax
import jax.numpy as jnp
from jax import lax
from jax.sharding import Mesh, PartitionSpec as P

H = 32
KV = 8
HD = 128
SWAP = [(0, 1), (1, 0)]
BLK = ("xl", "z", "c")


def contract_last(left, right):
    return lax.dot_general(
        left, right, (((1,), (1,)), ((), ())), preferred_element_type=jnp.float32
    )


def contract_first(left, right):
    return lax.dot_general(
        left, right, (((0,), (0,)), ((), ())), preferred_element_type=jnp.float32
    )


def head_pass(queries, cache_keys, cache_values, fresh_keys, fresh_values, grad_heads, offset):
    groups, row_count, head_width = queries.shape
    cached = cache_keys.shape[0]
    factor = head_width ** (-0.5)
    key_list = jnp.concatenate([cache_keys, fresh_keys], 0)
    value_list = jnp.concatenate([cache_values, fresh_values], 0)
    flat_query = queries.reshape(groups * row_count, head_width)
    flat_grad = grad_heads.reshape(groups * row_count, head_width)
    scores = contract_last(flat_query, key_list) * factor
    scores = scores.reshape(groups, row_count, cached + row_count)
    row_pos = lax.iota(jnp.int32, row_count)
    cache_ok = jnp.broadcast_to(lax.iota(jnp.int32, cached)[None, :] < offset, (row_count, cached))
    own_ok = row_pos[None, :] <= row_pos[:, None]
    allowed = jnp.concatenate([cache_ok, own_ok], 1)
    scores = jnp.where(allowed[None], scores, -jnp.inf)
    row_max = jnp.max(scores, axis=-1, keepdims=True)
    expo = jnp.exp(scores - row_max)
    probs = (expo / jnp.sum(expo, axis=-1, keepdims=True)).astype(jnp.bfloat16)
    probs = probs.reshape(groups * row_count, cached + row_count)
    attended = jnp.dot(probs, value_list, preferred_element_type=jnp.float32).astype(jnp.bfloat16)
    grad_probs = contract_last(flat_grad, value_list)
    probs_wide = probs.astype(jnp.float32)
    row_dot = jnp.sum(probs_wide * grad_probs, axis=-1, keepdims=True)
    grad_scores = (probs_wide * (grad_probs - row_dot) * factor).astype(jnp.bfloat16)
    grad_query = jnp.dot(grad_scores, key_list, preferred_element_type=jnp.float32).astype(
        jnp.bfloat16
    )
    grad_keys = contract_first(grad_scores[:, cached:], flat_query).astype(jnp.bfloat16)
    grad_values = contract_first(probs[:, cached:], flat_grad).astype(jnp.bfloat16)
    return (
        attended.reshape(groups, row_count, head_width),
        grad_query.reshape(groups, row_count, head_width),
        grad_keys,
        grad_values,
    )


def gather_rows(block):
    rows, width = block.shape
    z_count = lax.axis_size("z")
    x_pos = lax.axis_index("xl")
    z_pos = lax.axis_index("z")
    chip_core = lax.axis_index("c")
    peer = lax.ppermute(block, "xl", SWAP)
    pair = jnp.stack([jnp.where(x_pos == 0, block, peer), jnp.where(x_pos == 0, peer, block)])
    ahead = [(i, (i + 1) % z_count) for i in range(z_count)]
    behind = [(i, (i - 1) % z_count) for i in range(z_count)]
    ring = jnp.zeros((z_count,) + pair.shape, pair.dtype)
    ring = lax.dynamic_update_index_in_dim(ring, pair, z_pos, 0)
    fwd = pair
    bwd = pair
    for step in range(1, z_count // 2 + 1):
        fwd = lax.ppermute(fwd, "z", ahead)
        ring = lax.dynamic_update_index_in_dim(ring, fwd, (z_pos - step) % z_count, 0)
        if step < z_count - z_count // 2:
            bwd = lax.ppermute(bwd, "z", behind)
            ring = lax.dynamic_update_index_in_dim(ring, bwd, (z_pos + step) % z_count, 0)
    other = lax.ppermute(ring, "c", SWAP)
    first = jnp.where(chip_core == 0, ring, other)
    second = jnp.where(chip_core == 0, other, ring)
    full = jnp.stack([first, second], 2)
    return full.transpose(1, 0, 2, 3, 4).reshape(-1, width)


def local(hidden_in, w_query, w_key, w_value, starts, key_cache, value_cache, grad_out):
    tokens_dev = hidden_in.shape[0]
    kv_local = w_key.shape[1] // HD
    group = H // KV
    cached = key_cache.shape[1]
    query_cols = w_query.shape[1]
    kv_cols = w_key.shape[1]
    local_w = jnp.concatenate([w_query, w_key, w_value], 1)
    full_w = gather_rows(local_w)
    proj = jnp.dot(hidden_in, full_w, preferred_element_type=jnp.float32)
    queries = proj[:, :query_cols].astype(jnp.bfloat16)
    new_keys = proj[:, query_cols : query_cols + kv_cols].astype(jnp.bfloat16)
    new_values = proj[:, query_cols + kv_cols :].astype(jnp.bfloat16)
    per_query = queries.reshape(tokens_dev, kv_local, group, HD).transpose(1, 2, 0, 3)
    per_grad = grad_out.reshape(tokens_dev, kv_local, group, HD).transpose(1, 2, 0, 3)
    cache_k = key_cache[0].reshape(cached, kv_local, HD).transpose(1, 0, 2)
    cache_v = value_cache[0].reshape(cached, kv_local, HD).transpose(1, 0, 2)
    fresh_k = new_keys.reshape(tokens_dev, kv_local, HD).transpose(1, 0, 2)
    fresh_v = new_values.reshape(tokens_dev, kv_local, HD).transpose(1, 0, 2)
    offset = starts[0]
    results = lax.map(
        lambda packed: head_pass(*packed, offset),
        (per_query, cache_k, cache_v, fresh_k, fresh_v, per_grad),
    )
    attended = results[0].transpose(2, 0, 1, 3).reshape(tokens_dev, kv_local * group * HD)
    grad_query = results[1].transpose(2, 0, 1, 3).reshape(tokens_dev, kv_local * group * HD)
    grad_keys = results[2].transpose(1, 0, 2).reshape(tokens_dev, kv_local * HD)
    grad_values = results[3].transpose(1, 0, 2).reshape(tokens_dev, kv_local * HD)
    grads_cat = jnp.concatenate([grad_query, grad_keys, grad_values], 1)
    tp_count = lax.axis_size("tp")
    z_count = lax.axis_size("z")
    rows = w_query.shape[0]
    chip_core = lax.axis_index("c")
    x_pos = lax.axis_index("xl")
    by_place = hidden_in.reshape(tokens_dev, 2, z_count, 2, rows).transpose(0, 2, 1, 3, 4)
    cols_other = lax.dynamic_index_in_dim(by_place, 1 - chip_core, 3, False)
    cols_own = lax.dynamic_index_in_dim(by_place, chip_core, 3, False)
    part_other = contract_first(cols_other.reshape(tokens_dev, -1), grads_cat)
    from_peer = lax.ppermute(part_other.astype(jnp.bfloat16), "c", SWAP)
    from_peer, attended = lax.optimization_barrier((from_peer, attended))
    part_own = contract_first(cols_own.reshape(tokens_dev, -1), grads_cat)
    chip_sum = (part_own + from_peer.astype(jnp.float32)).astype(jnp.bfloat16)
    ring_sum = lax.psum_scatter(chip_sum, "z", scatter_dimension=0, tiled=True)
    ring_sum = ring_sum.reshape(2, rows, -1)
    keep = lax.dynamic_index_in_dim(ring_sum, x_pos, 0, False)
    give = lax.dynamic_index_in_dim(ring_sum, 1 - x_pos, 0, False)
    summed = keep.astype(jnp.float32) + lax.ppermute(give, "xl", SWAP).astype(jnp.float32)
    input_term = contract_last(grads_cat, full_w).astype(jnp.bfloat16)
    input_term = input_term.reshape(tokens_dev, tp_count, -1).transpose(1, 0, 2)
    gathered = lax.all_to_all(input_term, "tp", 0, 0, tiled=True)
    grad_in = jnp.sum(gathered.astype(jnp.float32), axis=0).astype(jnp.bfloat16)
    summed = summed * (tokens_dev * lax.axis_size(BLK)) ** (-0.5)
    grad_wq = summed[:, :query_cols]
    grad_wk = summed[:, query_cols : query_cols + kv_cols]
    grad_wv = summed[:, query_cols + kv_cols :]
    return (attended, grad_in, grad_wq, grad_wk, grad_wv)


def solution(mesh):
    blk = mesh.shape["blk"]
    devices = mesh.devices.reshape(2, blk // 4, 2, mesh.shape["tp"])
    split = Mesh(devices, BLK + ("tp",))
    in_specs = (
        P(BLK, None),
        P(BLK, "tp"),
        P(BLK, "tp"),
        P(BLK, "tp"),
        P(BLK),
        P(BLK, None, "tp"),
        P(BLK, None, "tp"),
        P(BLK, "tp"),
    )
    out_specs = (P(BLK, "tp"),) * 5
    return jax.shard_map(local, mesh=split, in_specs=in_specs, out_specs=out_specs, check_vma=False)
```

```python
import jax
import jax.numpy as jnp
from jax import lax
from jax.sharding import Mesh, PartitionSpec as P

H = 32
KV = 8
HD = 128
SWAP = [(0, 1), (1, 0)]
BLK = ("xl", "z", "c")


def contract_last(left, right):
    return lax.dot_general(
        left, right, (((1,), (1,)), ((), ())), preferred_element_type=jnp.float32
    )


def contract_first(left, right):
    return lax.dot_general(
        left, right, (((0,), (0,)), ((), ())), preferred_element_type=jnp.float32
    )


def head_pass(queries, cache_keys, cache_values, fresh_keys, fresh_values, grad_heads, offset):
    groups, row_count, head_width = queries.shape
    cached = cache_keys.shape[0]
    factor = head_width ** (-0.5)
    key_list = jnp.concatenate([cache_keys, fresh_keys], 0)
    value_list = jnp.concatenate([cache_values, fresh_values], 0)
    flat_query = queries.reshape(groups * row_count, head_width)
    flat_grad = grad_heads.reshape(groups * row_count, head_width)
    scores = contract_last(flat_query, key_list) * factor
    scores = scores.reshape(groups, row_count, cached + row_count)
    row_pos = lax.iota(jnp.int32, row_count)
    cache_ok = jnp.broadcast_to(lax.iota(jnp.int32, cached)[None, :] < offset, (row_count, cached))
    own_ok = row_pos[None, :] <= row_pos[:, None]
    allowed = jnp.concatenate([cache_ok, own_ok], 1)
    scores = jnp.where(allowed[None], scores, -jnp.inf)
    row_max = jnp.max(scores, axis=-1, keepdims=True)
    expo = jnp.exp(scores - row_max)
    probs = (expo / jnp.sum(expo, axis=-1, keepdims=True)).astype(jnp.bfloat16)
    probs = probs.reshape(groups * row_count, cached + row_count)
    attended = jnp.dot(probs, value_list, preferred_element_type=jnp.float32).astype(jnp.bfloat16)
    grad_probs = contract_last(flat_grad, value_list)
    probs_wide = probs.astype(jnp.float32)
    row_dot = jnp.sum(probs_wide * grad_probs, axis=-1, keepdims=True)
    grad_scores = (probs_wide * (grad_probs - row_dot) * factor).astype(jnp.bfloat16)
    grad_query = jnp.dot(grad_scores, key_list, preferred_element_type=jnp.float32).astype(
        jnp.bfloat16
    )
    grad_keys = contract_first(grad_scores[:, cached:], flat_query).astype(jnp.bfloat16)
    grad_values = contract_first(probs[:, cached:], flat_grad).astype(jnp.bfloat16)
    return (
        attended.reshape(groups, row_count, head_width),
        grad_query.reshape(groups, row_count, head_width),
        grad_keys,
        grad_values,
    )


def gather_rows(block):
    rows, width = block.shape
    z_count = lax.axis_size("z")
    x_pos = lax.axis_index("xl")
    z_pos = lax.axis_index("z")
    chip_core = lax.axis_index("c")
    peer = lax.ppermute(block, "xl", SWAP)
    pair = jnp.stack([jnp.where(x_pos == 0, block, peer), jnp.where(x_pos == 0, peer, block)])
    ahead = [(i, (i + 1) % z_count) for i in range(z_count)]
    behind = [(i, (i - 1) % z_count) for i in range(z_count)]
    ring = jnp.zeros((z_count,) + pair.shape, pair.dtype)
    ring = lax.dynamic_update_index_in_dim(ring, pair, z_pos, 0)
    fwd = pair
    bwd = pair
    for step in range(1, z_count // 2 + 1):
        fwd = lax.ppermute(fwd, "z", ahead)
        ring = lax.dynamic_update_index_in_dim(ring, fwd, (z_pos - step) % z_count, 0)
        if step < z_count - z_count // 2:
            bwd = lax.ppermute(bwd, "z", behind)
            ring = lax.dynamic_update_index_in_dim(ring, bwd, (z_pos + step) % z_count, 0)
    other = lax.ppermute(ring, "c", SWAP)
    first = jnp.where(chip_core == 0, ring, other)
    second = jnp.where(chip_core == 0, other, ring)
    full = jnp.stack([first, second], 2)
    return ring.reshape(-1, width), other.reshape(-1, width), full.transpose(1, 0, 2, 3, 4).reshape(-1, width)


def local(hidden_in, w_query, w_key, w_value, starts, key_cache, value_cache, grad_out):
    tokens_dev = hidden_in.shape[0]
    kv_local = w_key.shape[1] // HD
    group = H // KV
    cached = key_cache.shape[1]
    query_cols = w_query.shape[1]
    kv_cols = w_key.shape[1]
    local_w = jnp.concatenate([w_query, w_key, w_value], 1)
    own_w, other_w, full_w = gather_rows(local_w)
    z_count = lax.axis_size("z")
    rows = w_query.shape[0]
    chip_core = lax.axis_index("c")
    by_place = hidden_in.reshape(tokens_dev, 2, z_count, 2, rows).transpose(0, 2, 1, 3, 4)
    cols_other = lax.dynamic_index_in_dim(by_place, 1 - chip_core, 3, False).reshape(tokens_dev, -1)
    cols_own = lax.dynamic_index_in_dim(by_place, chip_core, 3, False).reshape(tokens_dev, -1)
    proj = jnp.dot(cols_own, own_w, preferred_element_type=jnp.float32)
    proj = proj + jnp.dot(cols_other, other_w, preferred_element_type=jnp.float32)
    queries = proj[:, :query_cols].astype(jnp.bfloat16)
    new_keys = proj[:, query_cols : query_cols + kv_cols].astype(jnp.bfloat16)
    new_values = proj[:, query_cols + kv_cols :].astype(jnp.bfloat16)
    per_query = queries.reshape(tokens_dev, kv_local, group, HD).transpose(1, 2, 0, 3)
    per_grad = grad_out.reshape(tokens_dev, kv_local, group, HD).transpose(1, 2, 0, 3)
    cache_k = key_cache[0].reshape(cached, kv_local, HD).transpose(1, 0, 2)
    cache_v = value_cache[0].reshape(cached, kv_local, HD).transpose(1, 0, 2)
    fresh_k = new_keys.reshape(tokens_dev, kv_local, HD).transpose(1, 0, 2)
    fresh_v = new_values.reshape(tokens_dev, kv_local, HD).transpose(1, 0, 2)
    offset = starts[0]
    results = lax.map(
        lambda packed: head_pass(*packed, offset),
        (per_query, cache_k, cache_v, fresh_k, fresh_v, per_grad),
    )
    attended = results[0].transpose(2, 0, 1, 3).reshape(tokens_dev, kv_local * group * HD)
    grad_query = results[1].transpose(2, 0, 1, 3).reshape(tokens_dev, kv_local * group * HD)
    grad_keys = results[2].transpose(1, 0, 2).reshape(tokens_dev, kv_local * HD)
    grad_values = results[3].transpose(1, 0, 2).reshape(tokens_dev, kv_local * HD)
    grads_cat = jnp.concatenate([grad_query, grad_keys, grad_values], 1)
    tp_count = lax.axis_size("tp")
    x_pos = lax.axis_index("xl")
    part_other = contract_first(cols_other, grads_cat)
    from_peer = lax.ppermute(part_other.astype(jnp.bfloat16), "c", SWAP)
    from_peer, attended = lax.optimization_barrier((from_peer, attended))
    part_own = contract_first(cols_own, grads_cat)
    chip_sum = (part_own + from_peer.astype(jnp.float32)).astype(jnp.bfloat16)
    ring_sum = lax.psum_scatter(chip_sum, "z", scatter_dimension=0, tiled=True)
    ring_sum = ring_sum.reshape(2, rows, -1)
    keep = lax.dynamic_index_in_dim(ring_sum, x_pos, 0, False)
    give = lax.dynamic_index_in_dim(ring_sum, 1 - x_pos, 0, False)
    summed = keep.astype(jnp.float32) + lax.ppermute(give, "xl", SWAP).astype(jnp.float32)
    input_term = contract_last(grads_cat, full_w).astype(jnp.bfloat16)
    input_term = input_term.reshape(tokens_dev, tp_count, -1).transpose(1, 0, 2)
    gathered = lax.all_to_all(input_term, "tp", 0, 0, tiled=True)
    grad_in = jnp.sum(gathered.astype(jnp.float32), axis=0).astype(jnp.bfloat16)
    summed = summed * (tokens_dev * lax.axis_size(BLK)) ** (-0.5)
    grad_wq = summed[:, :query_cols]
    grad_wk = summed[:, query_cols : query_cols + kv_cols]
    grad_wv = summed[:, query_cols + kv_cols :]
    return (attended, grad_in, grad_wq, grad_wk, grad_wv)


def solution(mesh):
    blk = mesh.shape["blk"]
    devices = mesh.devices.reshape(2, blk // 4, 2, mesh.shape["tp"])
    split = Mesh(devices, BLK + ("tp",))
    in_specs = (
        P(BLK, None),
        P(BLK, "tp"),
        P(BLK, "tp"),
        P(BLK, "tp"),
        P(BLK),
        P(BLK, None, "tp"),
        P(BLK, None, "tp"),
        P(BLK, "tp"),
    )
    out_specs = (P(BLK, "tp"),) * 5
    return jax.shard_map(local, mesh=split, in_specs=in_specs, out_specs=out_specs, check_vma=False)
```

```python
import jax
import jax.numpy as jnp
from jax import lax
from jax.sharding import Mesh, PartitionSpec as P

H = 32
KV = 8
HD = 128
SWAP = [(0, 1), (1, 0)]
BLK = ("xl", "z", "c")


def contract_last(left, right):
    return lax.dot_general(
        left, right, (((1,), (1,)), ((), ())), preferred_element_type=jnp.float32
    )


def contract_first(left, right):
    return lax.dot_general(
        left, right, (((0,), (0,)), ((), ())), preferred_element_type=jnp.float32
    )


def head_pass(queries, cache_keys, cache_values, fresh_keys, fresh_values, grad_heads, offset):
    groups, row_count, head_width = queries.shape
    cached = cache_keys.shape[0]
    factor = head_width ** (-0.5)
    key_list = jnp.concatenate([cache_keys, fresh_keys], 0)
    value_list = jnp.concatenate([cache_values, fresh_values], 0)
    flat_query = queries.reshape(groups * row_count, head_width)
    flat_grad = grad_heads.reshape(groups * row_count, head_width)
    scores = contract_last(flat_query, key_list) * factor
    scores = scores.reshape(groups, row_count, cached + row_count)
    row_pos = lax.iota(jnp.int32, row_count)
    cache_ok = jnp.broadcast_to(lax.iota(jnp.int32, cached)[None, :] < offset, (row_count, cached))
    own_ok = row_pos[None, :] <= row_pos[:, None]
    allowed = jnp.concatenate([cache_ok, own_ok], 1)
    scores = jnp.where(allowed[None], scores, -jnp.inf)
    row_max = jnp.max(scores, axis=-1, keepdims=True)
    expo = jnp.exp(scores - row_max)
    probs = (expo / jnp.sum(expo, axis=-1, keepdims=True)).astype(jnp.bfloat16)
    probs = probs.reshape(groups * row_count, cached + row_count)
    attended = jnp.dot(probs, value_list, preferred_element_type=jnp.float32).astype(jnp.bfloat16)
    grad_probs = contract_last(flat_grad, value_list)
    probs_wide = probs.astype(jnp.float32)
    row_dot = jnp.sum(probs_wide * grad_probs, axis=-1, keepdims=True)
    grad_scores = (probs_wide * (grad_probs - row_dot) * factor).astype(jnp.bfloat16)
    grad_query = jnp.dot(grad_scores, key_list, preferred_element_type=jnp.float32).astype(
        jnp.bfloat16
    )
    grad_keys = contract_first(grad_scores[:, cached:], flat_query).astype(jnp.bfloat16)
    grad_values = contract_first(probs[:, cached:], flat_grad).astype(jnp.bfloat16)
    return (
        attended.reshape(groups, row_count, head_width),
        grad_query.reshape(groups, row_count, head_width),
        grad_keys,
        grad_values,
    )


def gather_rows(block):
    rows, width = block.shape
    z_count = lax.axis_size("z")
    x_pos = lax.axis_index("xl")
    z_pos = lax.axis_index("z")
    chip_core = lax.axis_index("c")
    peer = lax.ppermute(block, "xl", SWAP)
    pair = jnp.stack([jnp.where(x_pos == 0, block, peer), jnp.where(x_pos == 0, peer, block)])
    ahead = [(i, (i + 1) % z_count) for i in range(z_count)]
    behind = [(i, (i - 1) % z_count) for i in range(z_count)]
    ring = jnp.zeros((z_count,) + pair.shape, pair.dtype)
    ring = lax.dynamic_update_index_in_dim(ring, pair, z_pos, 0)
    fwd = pair
    bwd = pair
    for step in range(1, z_count // 2 + 1):
        fwd = lax.ppermute(fwd, "z", ahead)
        ring = lax.dynamic_update_index_in_dim(ring, fwd, (z_pos - step) % z_count, 0)
        if step < z_count - z_count // 2:
            bwd = lax.ppermute(bwd, "z", behind)
            ring = lax.dynamic_update_index_in_dim(ring, bwd, (z_pos + step) % z_count, 0)
    other = lax.ppermute(ring, "c", SWAP)
    first = jnp.where(chip_core == 0, ring, other)
    second = jnp.where(chip_core == 0, other, ring)
    full = jnp.stack([first, second], 2)
    return ring.reshape(-1, width), other.reshape(-1, width), full.transpose(1, 0, 2, 3, 4).reshape(-1, width)


def local(hidden_in, w_query, w_key, w_value, starts, key_cache, value_cache, grad_out):
    tokens_dev = hidden_in.shape[0]
    kv_local = w_key.shape[1] // HD
    group = H // KV
    cached = key_cache.shape[1]
    query_cols = w_query.shape[1]
    kv_cols = w_key.shape[1]
    local_w = jnp.concatenate([w_query, w_key, w_value], 1)
    own_w, other_w, full_w = gather_rows(local_w)
    z_count = lax.axis_size("z")
    rows = w_query.shape[0]
    chip_core = lax.axis_index("c")
    by_place = hidden_in.reshape(tokens_dev, 2, z_count, 2, rows).transpose(0, 2, 1, 3, 4)
    cols_other = lax.dynamic_index_in_dim(by_place, 1 - chip_core, 3, False).reshape(tokens_dev, -1)
    cols_own = lax.dynamic_index_in_dim(by_place, chip_core, 3, False).reshape(tokens_dev, -1)
    proj = jnp.dot(cols_own, own_w, preferred_element_type=jnp.float32)
    proj = proj + jnp.dot(cols_other, other_w, preferred_element_type=jnp.float32)
    queries = proj[:, :query_cols].astype(jnp.bfloat16)
    new_keys = proj[:, query_cols : query_cols + kv_cols].astype(jnp.bfloat16)
    new_values = proj[:, query_cols + kv_cols :].astype(jnp.bfloat16)
    per_query = queries.reshape(tokens_dev, kv_local, group, HD).transpose(1, 2, 0, 3)
    per_grad = grad_out.reshape(tokens_dev, kv_local, group, HD).transpose(1, 2, 0, 3)
    cache_k = key_cache[0].reshape(cached, kv_local, HD).transpose(1, 0, 2)
    cache_v = value_cache[0].reshape(cached, kv_local, HD).transpose(1, 0, 2)
    fresh_k = new_keys.reshape(tokens_dev, kv_local, HD).transpose(1, 0, 2)
    fresh_v = new_values.reshape(tokens_dev, kv_local, HD).transpose(1, 0, 2)
    offset = starts[0]
    results = lax.map(
        lambda packed: head_pass(*packed, offset),
        (per_query, cache_k, cache_v, fresh_k, fresh_v, per_grad),
    )
    attended = results[0].transpose(2, 0, 1, 3).reshape(tokens_dev, kv_local * group * HD)
    grad_query = results[1].transpose(2, 0, 1, 3).reshape(tokens_dev, kv_local * group * HD)
    grad_keys = results[2].transpose(1, 0, 2).reshape(tokens_dev, kv_local * HD)
    grad_values = results[3].transpose(1, 0, 2).reshape(tokens_dev, kv_local * HD)
    grads_cat = jnp.concatenate([grad_query, grad_keys, grad_values], 1)
    tp_count = lax.axis_size("tp")
    x_pos = lax.axis_index("xl")
    part_other = contract_first(cols_other, grads_cat)
    from_peer = lax.ppermute(part_other.astype(jnp.bfloat16), "c", SWAP)
    from_peer, attended = lax.optimization_barrier((from_peer, attended))
    part_own = contract_first(cols_own, grads_cat)
    chip_sum = (part_own + from_peer.astype(jnp.float32)).astype(jnp.bfloat16)
    ring_sum = lax.psum_scatter(chip_sum, "z", scatter_dimension=0, tiled=True)
    ring_sum = ring_sum.reshape(2, rows, -1)
    from_x = lax.ppermute(ring_sum, "xl", SWAP)
    keep = lax.dynamic_index_in_dim(ring_sum, x_pos, 0, False)
    summed = keep.astype(jnp.float32) + lax.dynamic_index_in_dim(from_x, x_pos, 0, False).astype(jnp.float32)
    by_target = full_w.reshape(tp_count, -1, full_w.shape[1])
    input_term = jnp.einsum(
        "tk,cjk->ctj", grads_cat, by_target, preferred_element_type=jnp.float32
    ).astype(jnp.bfloat16)
    gathered = lax.all_to_all(input_term, "tp", 0, 0, tiled=True)
    grad_in = jnp.sum(gathered.astype(jnp.float32), axis=0).astype(jnp.bfloat16)
    summed = summed * (tokens_dev * lax.axis_size(BLK)) ** (-0.5)
    grad_wq = summed[:, :query_cols]
    grad_wk = summed[:, query_cols : query_cols + kv_cols]
    grad_wv = summed[:, query_cols + kv_cols :]
    return (attended, grad_in, grad_wq, grad_wk, grad_wv)


def solution(mesh):
    blk = mesh.shape["blk"]
    devices = mesh.devices.reshape(2, blk // 4, 2, mesh.shape["tp"])
    split = Mesh(devices, BLK + ("tp",))
    in_specs = (
        P(BLK, None),
        P(BLK, "tp"),
        P(BLK, "tp"),
        P(BLK, "tp"),
        P(BLK),
        P(BLK, None, "tp"),
        P(BLK, None, "tp"),
        P(BLK, "tp"),
    )
    out_specs = (P(BLK, "tp"),) * 5
    return jax.shard_map(local, mesh=split, in_specs=in_specs, out_specs=out_specs, check_vma=False)
```

```python
import jax
import jax.numpy as jnp
from jax import lax
from jax.sharding import Mesh, PartitionSpec as P

H = 32
KV = 8
HD = 128
SWAP = [(0, 1), (1, 0)]
BLK = ("xl", "z", "c")


def contract_last(left, right):
    return lax.dot_general(
        left, right, (((1,), (1,)), ((), ())), preferred_element_type=jnp.float32
    )


def contract_first(left, right):
    return lax.dot_general(
        left, right, (((0,), (0,)), ((), ())), preferred_element_type=jnp.float32
    )


def head_pass(queries, cache_keys, cache_values, fresh_keys, fresh_values, grad_heads, offset):
    groups, row_count, head_width = queries.shape
    cached = cache_keys.shape[0]
    factor = head_width ** (-0.5)
    key_list = jnp.concatenate([cache_keys, fresh_keys], 0)
    value_list = jnp.concatenate([cache_values, fresh_values], 0)
    flat_query = queries.reshape(groups * row_count, head_width)
    flat_grad = grad_heads.reshape(groups * row_count, head_width)
    scores = contract_last(flat_query, key_list) * factor
    scores = scores.reshape(groups, row_count, cached + row_count)
    row_pos = lax.iota(jnp.int32, row_count)
    cache_ok = jnp.broadcast_to(lax.iota(jnp.int32, cached)[None, :] < offset, (row_count, cached))
    own_ok = row_pos[None, :] <= row_pos[:, None]
    allowed = jnp.concatenate([cache_ok, own_ok], 1)
    scores = jnp.where(allowed[None], scores, -jnp.inf)
    row_max = jnp.max(scores, axis=-1, keepdims=True)
    expo = jnp.exp(scores - row_max)
    probs = (expo / jnp.sum(expo, axis=-1, keepdims=True)).astype(jnp.bfloat16)
    probs = probs.reshape(groups * row_count, cached + row_count)
    attended = jnp.dot(probs, value_list, preferred_element_type=jnp.float32).astype(jnp.bfloat16)
    grad_probs = contract_last(flat_grad, value_list)
    probs_wide = probs.astype(jnp.float32)
    row_dot = jnp.sum(probs_wide * grad_probs, axis=-1, keepdims=True)
    grad_scores = (probs_wide * (grad_probs - row_dot) * factor).astype(jnp.bfloat16)
    grad_query = jnp.dot(grad_scores, key_list, preferred_element_type=jnp.float32).astype(
        jnp.bfloat16
    )
    grad_keys = contract_first(grad_scores[:, cached:], flat_query).astype(jnp.bfloat16)
    grad_values = contract_first(probs[:, cached:], flat_grad).astype(jnp.bfloat16)
    return (
        attended.reshape(groups, row_count, head_width),
        grad_query.reshape(groups, row_count, head_width),
        grad_keys,
        grad_values,
    )


def gather_rows(block):
    rows, width = block.shape
    z_count = lax.axis_size("z")
    x_pos = lax.axis_index("xl")
    z_pos = lax.axis_index("z")
    chip_core = lax.axis_index("c")
    peer = lax.ppermute(block, "xl", SWAP)
    pair = jnp.stack([jnp.where(x_pos == 0, block, peer), jnp.where(x_pos == 0, peer, block)])
    ahead = [(i, (i + 1) % z_count) for i in range(z_count)]
    behind = [(i, (i - 1) % z_count) for i in range(z_count)]
    ring = jnp.zeros((z_count,) + pair.shape, pair.dtype)
    ring = lax.dynamic_update_index_in_dim(ring, pair, z_pos, 0)
    fwd = pair
    bwd = pair
    for step in range(1, z_count // 2 + 1):
        fwd = lax.ppermute(fwd, "z", ahead)
        ring = lax.dynamic_update_index_in_dim(ring, fwd, (z_pos - step) % z_count, 0)
        if step < z_count - z_count // 2:
            bwd = lax.ppermute(bwd, "z", behind)
            ring = lax.dynamic_update_index_in_dim(ring, bwd, (z_pos + step) % z_count, 0)
    other = lax.ppermute(ring, "c", SWAP)
    first = jnp.where(chip_core == 0, ring, other)
    second = jnp.where(chip_core == 0, other, ring)
    full = jnp.stack([first, second], 2)
    return ring.reshape(-1, width), other.reshape(-1, width), full.transpose(1, 0, 2, 3, 4).reshape(-1, width)


def local(hidden_in, w_query, w_key, w_value, starts, key_cache, value_cache, grad_out):
    tokens_dev = hidden_in.shape[0]
    kv_local = w_key.shape[1] // HD
    group = H // KV
    cached = key_cache.shape[1]
    query_cols = w_query.shape[1]
    kv_cols = w_key.shape[1]
    local_w = jnp.concatenate([w_query, w_key, w_value], 1)
    own_w, other_w, full_w = gather_rows(local_w)
    z_count = lax.axis_size("z")
    rows = w_query.shape[0]
    chip_core = lax.axis_index("c")
    by_place = hidden_in.reshape(tokens_dev, 2, z_count, 2, rows).transpose(0, 2, 1, 3, 4)
    cols_other = lax.dynamic_index_in_dim(by_place, 1 - chip_core, 3, False).reshape(tokens_dev, -1)
    cols_own = lax.dynamic_index_in_dim(by_place, chip_core, 3, False).reshape(tokens_dev, -1)
    proj = jnp.dot(cols_own, own_w, preferred_element_type=jnp.float32)
    proj = proj + jnp.dot(cols_other, other_w, preferred_element_type=jnp.float32)
    queries = proj[:, :query_cols].astype(jnp.bfloat16)
    new_keys = proj[:, query_cols : query_cols + kv_cols].astype(jnp.bfloat16)
    new_values = proj[:, query_cols + kv_cols :].astype(jnp.bfloat16)
    per_query = queries.reshape(tokens_dev, kv_local, group, HD).transpose(1, 2, 0, 3)
    per_grad = grad_out.reshape(tokens_dev, kv_local, group, HD).transpose(1, 2, 0, 3)
    cache_k = key_cache[0].reshape(cached, kv_local, HD).transpose(1, 0, 2)
    cache_v = value_cache[0].reshape(cached, kv_local, HD).transpose(1, 0, 2)
    fresh_k = new_keys.reshape(tokens_dev, kv_local, HD).transpose(1, 0, 2)
    fresh_v = new_values.reshape(tokens_dev, kv_local, HD).transpose(1, 0, 2)
    offset = starts[0]
    results = lax.map(
        lambda packed: head_pass(*packed, offset),
        (per_query, cache_k, cache_v, fresh_k, fresh_v, per_grad),
    )
    attended = results[0].transpose(2, 0, 1, 3).reshape(tokens_dev, kv_local * group * HD)
    grad_query = results[1].transpose(2, 0, 1, 3).reshape(tokens_dev, kv_local * group * HD)
    grad_keys = results[2].transpose(1, 0, 2).reshape(tokens_dev, kv_local * HD)
    grad_values = results[3].transpose(1, 0, 2).reshape(tokens_dev, kv_local * HD)
    grads_cat = jnp.concatenate([grad_query, grad_keys, grad_values], 1)
    tp_count = lax.axis_size("tp")
    x_pos = lax.axis_index("xl")
    part_other = contract_first(cols_other, grads_cat)
    from_peer = lax.ppermute(part_other.astype(jnp.bfloat16), "c", SWAP)
    from_peer, attended = lax.optimization_barrier((from_peer, attended))
    part_own = contract_first(cols_own, grads_cat)
    chip_sum = (part_own + from_peer.astype(jnp.float32)).astype(jnp.bfloat16)
    ring_sum = lax.psum_scatter(chip_sum, "z", scatter_dimension=0, tiled=True)
    ring_sum = ring_sum.reshape(2, rows, -1)
    from_x = lax.ppermute(ring_sum, "xl", SWAP)
    keep = lax.dynamic_index_in_dim(ring_sum, x_pos, 0, False)
    summed = keep.astype(jnp.float32) + lax.dynamic_index_in_dim(from_x, x_pos, 0, False).astype(jnp.float32)
    input_term = contract_last(grads_cat, full_w).astype(jnp.bfloat16)
    input_term = input_term.reshape(tokens_dev, tp_count, -1).transpose(1, 0, 2)
    gathered = lax.all_to_all(input_term, "tp", 0, 0, tiled=True)
    grad_in = jnp.sum(gathered.astype(jnp.float32), axis=0).astype(jnp.bfloat16)
    summed = summed * (tokens_dev * lax.axis_size(BLK)) ** (-0.5)
    grad_wq = summed[:, :query_cols]
    grad_wk = summed[:, query_cols : query_cols + kv_cols]
    grad_wv = summed[:, query_cols + kv_cols :]
    return (attended, grad_in, grad_wq, grad_wk, grad_wv)


def solution(mesh):
    blk = mesh.shape["blk"]
    devices = mesh.devices.reshape(2, blk // 4, 2, mesh.shape["tp"])
    split = Mesh(devices, BLK + ("tp",))
    in_specs = (
        P(BLK, None),
        P(BLK, "tp"),
        P(BLK, "tp"),
        P(BLK, "tp"),
        P(BLK),
        P(BLK, None, "tp"),
        P(BLK, None, "tp"),
        P(BLK, "tp"),
    )
    out_specs = (P(BLK, "tp"),) * 5
    return jax.shard_map(local, mesh=split, in_specs=in_specs, out_specs=out_specs, check_vma=False)
```
